512 devices in a mesh: gx: 16 (over z_hi, x), gy: 8 (over y, core), gz: 4 (over z_lo).
Axes of the slice: x: 4, y: 4, z: 16 (z_hi: 4, z_lo: 4; z = z_hi * 4 + z_lo), core: 2. Of those that a mesh axis runs over, the one named last changes fastest.
Arguments:
- features: bfloat16 [16, 8, 4, 4096, 128], P('gx', 'gy', 'gz'), may hold values from -6 to 6
- output_grad: bfloat16 [16, 8, 4, 4096, 128], P('gx', 'gy', 'gz'), may hold values from -6 to 6
- kernel: bfloat16 [27, 128, 128], replicated, may hold values from -0.5 to 0.5
- inner_map: int32 [16, 8, 4, 288, 3], P('gx', 'gy', 'gz'), may hold values from 0 to 31, as said below
- outer_map: int32 [16, 8, 4, 32, 3], P('gx', 'gy', 'gz'), may hold values from 0 to 55, as said below
- face_blocks: int32 [16, 8, 4, 3, 2, 4], P('gx', 'gy', 'gz'), may hold values from 0 to 31, as said below
- inner_live: int32 [16, 8, 4], P('gx', 'gy', 'gz'), may hold values from 72 to 288, as said below
- outer_live: int32 [16, 8, 4], P('gx', 'gy', 'gz'), may hold values from 16 to 32, as said below
Outputs:
- input_grad: bfloat16 [16, 8, 4, 4096, 128], P('gx', 'gy', 'gz')
- weight_grad: bfloat16 [27, 128, 128], replicated
The draws below stay inside these ranges and needn't reach their ends.
Inputs may be any that keep to these rules, and one draw needn't show every extreme that they name: `inner_map`: offsets lie in 0 to 26, output and input blocks in 0 to 31; every entry is valid, live or not. `outer_map`: offsets lie in 0 to 26, received blocks in 32 to 55, input blocks in 0 to 31; every entry is valid, live or not. Pairs may name a neighbour that does not exist; its blocks are zero. `face_blocks`: block indices of the brick itself; they may repeat. `inner_live`: some brick has all 288 entries live in every draw. `outer_live`: some brick has all 32 entries live in every draw.
All inputs are finite; a program needn't handle non-finite values.
Results may differ from the reference program's by a relative error of at most 0.001.
Values may be sent and summed in bfloat16 or wider, within the bound.
No kernel may reach another device: no remote copies, remote signals or barrier semaphores. Data moves between devices by JAX's collectives and lax.ppermute only.
A program may use at most 64 MiB of HBM per device.

```python
import math
import jax
import jax.numpy as jnp
from jax import lax

C = 128
BLOCK = 128
NB = 32
F = 4
PI = 288
PB = 32
ROWS = 4096
BX = 16
BY = 8
BZ = 4
BRICKS = 512


def draw_inner_map(key, part):
    keys = jax.random.split(jax.random.fold_in(key, 11), 3)
    shape_full = (BX, BY, BZ, PI)
    offsets = jax.random.randint(keys[0], shape_full, 0, 27)
    out_blocks = jax.random.randint(keys[1], shape_full, 0, NB)
    in_blocks = jax.random.randint(keys[2], shape_full, 0, NB)
    return jnp.stack([offsets, out_blocks, in_blocks], axis=-1).astype(jnp.int32)


def draw_outer_map(key, part):
    keys = jax.random.split(jax.random.fold_in(key, 12), 3)
    shape_full = (BX, BY, BZ, PB)
    offsets = jax.random.randint(keys[0], shape_full, 0, 27)
    out_blocks = jax.random.randint(keys[1], shape_full, NB, NB + 6 * F)
    in_blocks = jax.random.randint(keys[2], shape_full, 0, NB)
    return jnp.stack([offsets, out_blocks, in_blocks], axis=-1).astype(jnp.int32)


def draw_face_blocks(key, part):
    return jax.random.randint(jax.random.fold_in(key, 13), (BX, BY, BZ, 3, 2, F), 0, NB).astype(jnp.int32)


def draw_inner_live(key, part):
    keys = jax.random.split(jax.random.fold_in(key, 14), 2)
    counts = jax.random.randint(keys[0], (BRICKS,), PI // 4, PI + 1)
    chosen = jax.random.randint(keys[1], (), 0, BRICKS)
    counts = counts.at[chosen].set(PI)
    return counts.reshape(BX, BY, BZ).astype(jnp.int32)


def draw_outer_live(key, part):
    keys = jax.random.split(jax.random.fold_in(key, 15), 2)
    counts = jax.random.randint(keys[0], (BRICKS,), PB // 2, PB + 1)
    chosen = jax.random.randint(keys[1], (), 0, BRICKS)
    counts = counts.at[chosen].set(PB)
    return counts.reshape(BX, BY, BZ).astype(jnp.int32)


def block_levels(own_key, shape, cuts, least, high):
    def one(position, blocks):
        draws = jax.random.uniform(jax.random.fold_in(jax.random.fold_in(own_key, 6), position), (blocks,), jnp.float32, least / len(cuts), high / len(cuts))
        return jnp.repeat(jnp.exp(draws), shape[position] // blocks).reshape((-1,) + (1,) * (len(shape) - position - 1))

    level = one(*cuts[0])
    for cut in cuts[1:]:
        level = level * one(*cut)
    return level


def bell_draw(stream_key, shape, width, limit, cuts=(), held_as=jnp.bfloat16):
    values = width * jax.random.normal(stream_key, shape, jnp.float32)
    if cuts:
        values = values * block_levels(stream_key, shape, cuts, -0.22, 0.18)
    return jnp.clip(values, -limit, limit).astype(held_as)


def setup_inputs(seed: int = 0) -> dict:
    splits = jax.random.split(jax.random.key(seed), 9)
    features = bell_draw(splits[0], (BX, BY, BZ, ROWS, C), 1.0, 6.0, ((0, 16), (1, 8), (2, 4)))
    output_grad = bell_draw(splits[1], (BX, BY, BZ, ROWS, C), 1.0, 6.0, ((0, 16), (1, 8), (2, 4)))
    kernel = bell_draw(splits[2], (27, C, C), C ** -0.5, 0.5)
    inner_map = draw_inner_map(jax.random.fold_in(splits[8], 71), 0)
    outer_map = draw_outer_map(jax.random.fold_in(splits[8], 71), 0)
    face_blocks = draw_face_blocks(jax.random.fold_in(splits[8], 71), 0)
    inner_live = draw_inner_live(jax.random.fold_in(splits[8], 71), 0)
    outer_live = draw_outer_live(jax.random.fold_in(splits[8], 71), 0)
    return {"features": features, "output_grad": output_grad, "kernel": kernel, "inner_map": inner_map, "outer_map": outer_map, "face_blocks": face_blocks, "inner_live": inner_live, "outer_live": outer_live}


def brick_table(output_grad, face_blocks, brick_x, brick_y, brick_z):
    pieces = [output_grad[brick_x, brick_y, brick_z].reshape(NB, BLOCK, C)]
    limits = (BX, BY, BZ)
    for axis_index in range(3):
        for side_index, step_sign in ((0, -1), (1, 1)):
            coords = [brick_x, brick_y, brick_z]
            coords[axis_index] = coords[axis_index] + step_sign
            inside = (coords[axis_index] >= 0) & (coords[axis_index] < limits[axis_index])
            clipped = [jnp.clip(coords[0], 0, BX - 1), jnp.clip(coords[1], 0, BY - 1), jnp.clip(coords[2], 0, BZ - 1)]
            neighbour = output_grad[clipped[0], clipped[1], clipped[2]].reshape(NB, BLOCK, C)
            chosen = face_blocks[clipped[0], clipped[1], clipped[2], axis_index, 1 - side_index]
            blocks = neighbour[chosen]
            pieces.append(jnp.where(inside, blocks, jnp.zeros_like(blocks)))
    return jnp.concatenate(pieces, axis=0)

def reference(features, output_grad, kernel, inner_map, outer_map, face_blocks, inner_live, outer_live):

    def per_brick(weight_acc, brick_index):
        brick_x = brick_index // (BY * BZ)
        brick_y = brick_index // BZ % BY
        brick_z = brick_index % BZ
        gradient_table = brick_table(output_grad, face_blocks, brick_x, brick_y, brick_z)
        local_feats = features[brick_x, brick_y, brick_z].reshape(NB, BLOCK, C).astype(jnp.float32)
        pair_rows = jnp.concatenate([inner_map[brick_x, brick_y, brick_z], outer_map[brick_x, brick_y, brick_z]], axis=0)
        live_mask = jnp.concatenate([jnp.arange(PI, dtype=jnp.int32) < inner_live[brick_x, brick_y, brick_z], jnp.arange(PB, dtype=jnp.int32) < outer_live[brick_x, brick_y, brick_z]]).astype(jnp.float32)[:, None, None]
        offsets = pair_rows[:, 0]
        grad_rows = gradient_table[pair_rows[:, 1]].astype(jnp.float32)
        in_blocks = pair_rows[:, 2]
        kernels = kernel[offsets].astype(jnp.float32)
        backward = jnp.einsum('prd,pcd->prc', grad_rows, kernels) * live_mask
        input_acc = jnp.zeros((NB, BLOCK, C), jnp.float32).at[in_blocks].add(backward)
        outer_terms = jnp.einsum('prc,prd->pcd', local_feats[in_blocks], grad_rows) * live_mask
        weight_acc = weight_acc.at[offsets].add(outer_terms)
        return (weight_acc, input_acc.astype(jnp.bfloat16).reshape(ROWS, C))
    weight_sum, input_blocks = lax.scan(per_brick, jnp.zeros((27, C, C), jnp.float32), jnp.arange(BRICKS, dtype=jnp.int32))
    grad_scale = math.sqrt(27.0 / (BRICKS * PI * BLOCK))
    input_grad = input_blocks.reshape(BX, BY, BZ, ROWS, C)
    weight_grad = (weight_sum * grad_scale).astype(jnp.bfloat16)
    return (input_grad, weight_grad)
```

```python
import math

import jax
import jax.numpy as jnp
from jax import lax
from jax.experimental import pallas as pl
from jax.experimental.pallas import tpu as pltpu
from jax.sharding import PartitionSpec as P

C = 128
BLOCK = 128
NB = 32
PI = 288
PB = 32


def extended(shard, sides, width):
    for axis, dim in sides:
        count, length = (lax.axis_size(axis), shard.shape[dim])
        up = [(i, (i + 1) % count) for i in range(count - 1)]
        down = [(j, i) for i, j in up]
        last = lax.slice_in_dim(shard, length - width, length, axis=dim)
        initial = lax.slice_in_dim(shard, 0, width, axis=dim)
        before = lax.ppermute(last, axis, up)
        after = lax.ppermute(initial, axis, down)
        shard = jnp.concatenate([before, shard, after], axis=dim)
    return shard


def received_blocks(local_grads, face_lists):
    got_x = extended(local_grads[face_lists[0]], (("gx", 0),), 1)
    got_y = extended(local_grads[face_lists[1]], (("gy", 0),), 1)
    got_z = extended(local_grads[face_lists[2]], (("gz", 0),), 1)
    return jnp.concatenate(
        [got_x[0], got_x[3], got_y[0], got_y[3], got_z[0], got_z[3]], axis=0
    )


def pair_loop(pairs_ref, live_ref, table_ref, ft_ref, kt_ref, acc_in, acc_w, table_base):
    def one_pair(i, carry):
        k = pairs_ref[3 * i]
        a = pairs_ref[3 * i + 1] - table_base
        b = pairs_ref[3 * i + 2]
        g = table_ref[a]
        acc_in[b] += jnp.dot(g, kt_ref[k], preferred_element_type=jnp.float32)
        acc_w[k] += jnp.dot(ft_ref[b], g, preferred_element_type=jnp.float32)
        return carry

    lax.fori_loop(0, live_ref[0], one_pair, 0)


def inner_kernel(pairs_ref, live_ref, table_ref, ft_ref, kt_ref, acc_in, acc_w):
    acc_in[...] = jnp.zeros_like(acc_in)
    acc_w[...] = jnp.zeros_like(acc_w)
    pair_loop(pairs_ref, live_ref, table_ref, ft_ref, kt_ref, acc_in, acc_w, 0)


def outer_kernel(pairs_ref, live_ref, table_ref, ft_ref, kt_ref, in_start, w_start, grad_out, acc_w, acc_in):
    acc_in[...] = in_start[...]
    acc_w[...] = w_start[...]
    pair_loop(pairs_ref, live_ref, table_ref, ft_ref, kt_ref, acc_in, acc_w, NB)
    grad_out[...] = acc_in[...].astype(grad_out.dtype)


def vmem():
    return pl.BlockSpec(memory_space=pltpu.MemorySpace.VMEM)


def smem():
    return pl.BlockSpec(memory_space=pltpu.MemorySpace.SMEM)


def run_inner(pairs, live, table, ft, kt):
    n = pairs.shape[0] // 3
    return pl.pallas_call(
        inner_kernel,
        out_shape=(
            jax.ShapeDtypeStruct((NB, BLOCK, C), jnp.float32),
            jax.ShapeDtypeStruct((27, C, C), jnp.float32),
        ),
        in_specs=[smem(), smem(), vmem(), vmem(), vmem()],
        out_specs=(vmem(), vmem()),
        cost_estimate=pl.CostEstimate(
            flops=4 * n * BLOCK * C * C, transcendentals=0, bytes_accessed=8 * 1024 * 1024
        ),
        name="inner_pairs",
    )(pairs, live, table, ft, kt)


def run_outer(pairs, live, table, ft, kt, acc_in, acc_w):
    n = pairs.shape[0] // 3
    return pl.pallas_call(
        outer_kernel,
        out_shape=(
            jax.ShapeDtypeStruct((NB, BLOCK, C), jnp.bfloat16),
            jax.ShapeDtypeStruct((27, C, C), jnp.float32),
        ),
        in_specs=[smem(), smem(), vmem(), vmem(), vmem(), vmem(), vmem()],
        out_specs=(vmem(), vmem()),
        scratch_shapes=[pltpu.VMEM((NB, BLOCK, C), jnp.float32)],
        cost_estimate=pl.CostEstimate(
            flops=4 * n * BLOCK * C * C, transcendentals=0, bytes_accessed=8 * 1024 * 1024
        ),
        name="outer_pairs",
    )(pairs, live, table, ft, kt, acc_in, acc_w)


def reduce_weights(weight_acc, grad_scale):
    flat = weight_acc.reshape(-1)
    for axis in ("gy", "gz", "gx"):
        n = lax.axis_size(axis)
        parts = lax.all_to_all(flat.reshape(n, -1), axis, 0, 0, tiled=True)
        flat = parts.reshape(n, -1).sum(axis=0)
    piece = (flat * grad_scale).astype(jnp.bfloat16)
    n = lax.axis_size("gx")
    copies = jnp.broadcast_to(piece[None], (n,) + piece.shape)
    piece = lax.all_to_all(copies, "gx", 0, 0, tiled=True).reshape(-1)
    piece = lax.all_gather(piece, "gz", tiled=True)
    piece = lax.all_gather(piece, "gy", tiled=True)
    return piece.reshape(weight_acc.shape)


def body(features, output_grad, kernel, inner_map, outer_map, face_blocks, inner_live, outer_live):
    local_grads = output_grad[0, 0, 0].reshape(NB, BLOCK, C)
    feats_t = jnp.swapaxes(features[0, 0, 0].reshape(NB, BLOCK, C), 1, 2)
    kernel_t = jnp.swapaxes(kernel, 1, 2)
    inner_pairs = inner_map[0, 0, 0].reshape(-1)
    outer_pairs = outer_map[0, 0, 0].reshape(-1)
    inner_n = jnp.clip(inner_live[0, 0, 0], 0, PI).reshape(1)
    outer_n = jnp.clip(outer_live[0, 0, 0], 0, PB).reshape(1)
    received = received_blocks(local_grads, face_blocks[0, 0, 0])
    acc_in, acc_w = run_inner(inner_pairs, inner_n, local_grads, feats_t, kernel_t)
    input_grad, acc_w = run_outer(outer_pairs, outer_n, received, feats_t, kernel_t, acc_in, acc_w)
    bricks_all = lax.axis_size("gx") * lax.axis_size("gy") * lax.axis_size("gz")
    grad_scale = math.sqrt(27.0 / (bricks_all * PI * BLOCK))
    weight_grad = reduce_weights(acc_w, grad_scale)
    return (input_grad.reshape(1, 1, 1, NB * BLOCK, C), weight_grad)


def solution(mesh):
    in_specs = (
        P("gx", "gy", "gz", None, None),
        P("gx", "gy", "gz", None, None),
        P(),
        P("gx", "gy", "gz", None, None),
        P("gx", "gy", "gz", None, None),
        P("gx", "gy", "gz", None, None, None),
        P("gx", "gy", "gz"),
        P("gx", "gy", "gz"),
    )
    out_specs = (P("gx", "gy", "gz", None, None), P())
    return jax.shard_map(body, mesh=mesh, in_specs=in_specs, out_specs=out_specs, check_vma=False)
```

```python
import math

import jax
import jax.numpy as jnp
from jax import lax
from jax.experimental import pallas as pl
from jax.experimental.pallas import tpu as pltpu
from jax.sharding import PartitionSpec as P

C = 128
BLOCK = 128
NB = 32
PI = 288
PB = 32
UNROLL = 4


def extended(shard, sides, width):
    for axis, dim in sides:
        count, length = (lax.axis_size(axis), shard.shape[dim])
        up = [(i, (i + 1) % count) for i in range(count - 1)]
        down = [(j, i) for i, j in up]
        last = lax.slice_in_dim(shard, length - width, length, axis=dim)
        initial = lax.slice_in_dim(shard, 0, width, axis=dim)
        before = lax.ppermute(last, axis, up)
        after = lax.ppermute(initial, axis, down)
        shard = jnp.concatenate([before, shard, after], axis=dim)
    return shard


def received_blocks(local_grads, face_lists):
    got_x = extended(local_grads[face_lists[0]], (("gx", 0),), 1)
    got_y = extended(local_grads[face_lists[1]], (("gy", 0),), 1)
    got_z = extended(local_grads[face_lists[2]], (("gz", 0),), 1)
    return jnp.concatenate(
        [got_x[0], got_x[3], got_y[0], got_y[3], got_z[0], got_z[3]], axis=0
    )


def pair_loop(pairs_ref, live_ref, table_ref, ft_ref, kt_ref, acc_in, acc_w, table_base):
    def pair_ids(i):
        return (pairs_ref[3 * i], pairs_ref[3 * i + 1] - table_base, pairs_ref[3 * i + 2])

    def one_group(group, carry):
        ids = [pair_ids(group * UNROLL + j) for j in range(UNROLL)]
        grads = [table_ref[a] for _, a, _ in ids]
        to_in = [
            jnp.dot(g, kt_ref[k], preferred_element_type=jnp.float32)
            for g, (k, _, _) in zip(grads, ids)
        ]
        to_w = [
            jnp.dot(ft_ref[b], g, preferred_element_type=jnp.float32)
            for g, (_, _, b) in zip(grads, ids)
        ]
        for (k, _, b), p_in, p_w in zip(ids, to_in, to_w):
            acc_in[b] += p_in
            acc_w[k] += p_w
        return carry

    def one_pair(i, carry):
        k, a, b = pair_ids(i)
        g = table_ref[a]
        acc_in[b] += jnp.dot(g, kt_ref[k], preferred_element_type=jnp.float32)
        acc_w[k] += jnp.dot(ft_ref[b], g, preferred_element_type=jnp.float32)
        return carry

    live = live_ref[0]
    groups = live // UNROLL
    lax.fori_loop(0, groups, one_group, 0)
    lax.fori_loop(groups * UNROLL, live, one_pair, 0)


def inner_kernel(pairs_ref, live_ref, table_ref, ft_ref, kt_ref, acc_in, acc_w):
    acc_in[...] = jnp.zeros_like(acc_in)
    acc_w[...] = jnp.zeros_like(acc_w)
    pair_loop(pairs_ref, live_ref, table_ref, ft_ref, kt_ref, acc_in, acc_w, 0)


def outer_kernel(pairs_ref, live_ref, table_ref, ft_ref, kt_ref, in_start, w_start, grad_out, acc_w, acc_in):
    acc_in[...] = in_start[...]
    acc_w[...] = w_start[...]
    pair_loop(pairs_ref, live_ref, table_ref, ft_ref, kt_ref, acc_in, acc_w, NB)
    grad_out[...] = acc_in[...].astype(grad_out.dtype)


def vmem():
    return pl.BlockSpec(memory_space=pltpu.MemorySpace.VMEM)


def smem():
    return pl.BlockSpec(memory_space=pltpu.MemorySpace.SMEM)


def run_inner(pairs, live, table, ft, kt):
    n = pairs.shape[0] // 3
    return pl.pallas_call(
        inner_kernel,
        out_shape=(
            jax.ShapeDtypeStruct((NB, BLOCK, C), jnp.float32),
            jax.ShapeDtypeStruct((27, C, C), jnp.float32),
        ),
        in_specs=[smem(), smem(), vmem(), vmem(), vmem()],
        out_specs=(vmem(), vmem()),
        cost_estimate=pl.CostEstimate(
            flops=4 * n * BLOCK * C * C, transcendentals=0, bytes_accessed=8 * 1024 * 1024
        ),
        name="inner_pairs",
    )(pairs, live, table, ft, kt)


def run_outer(pairs, live, table, ft, kt, acc_in, acc_w):
    n = pairs.shape[0] // 3
    return pl.pallas_call(
        outer_kernel,
        out_shape=(
            jax.ShapeDtypeStruct((NB, BLOCK, C), jnp.bfloat16),
            jax.ShapeDtypeStruct((27, C, C), jnp.float32),
        ),
        in_specs=[smem(), smem(), vmem(), vmem(), vmem(), vmem(), vmem()],
        out_specs=(vmem(), vmem()),
        scratch_shapes=[pltpu.VMEM((NB, BLOCK, C), jnp.float32)],
        cost_estimate=pl.CostEstimate(
            flops=4 * n * BLOCK * C * C, transcendentals=0, bytes_accessed=8 * 1024 * 1024
        ),
        name="outer_pairs",
    )(pairs, live, table, ft, kt, acc_in, acc_w)


def reduce_weights(weight_acc, grad_scale):
    flat = weight_acc.reshape(-1)
    for axis in ("gy", "gz", "gx"):
        n = lax.axis_size(axis)
        parts = lax.all_to_all(flat.reshape(n, -1), axis, 0, 0, tiled=True)
        flat = parts.reshape(n, -1).sum(axis=0)
    piece = (flat * grad_scale).astype(jnp.bfloat16)
    n = lax.axis_size("gx")
    copies = jnp.broadcast_to(piece[None], (n,) + piece.shape)
    piece = lax.all_to_all(copies, "gx", 0, 0, tiled=True).reshape(-1)
    piece = lax.all_gather(piece, "gz", tiled=True)
    piece = lax.all_gather(piece, "gy", tiled=True)
    return piece.reshape(weight_acc.shape)


def body(features, output_grad, kernel, inner_map, outer_map, face_blocks, inner_live, outer_live):
    local_grads = output_grad[0, 0, 0].reshape(NB, BLOCK, C)
    feats_t = jnp.swapaxes(features[0, 0, 0].reshape(NB, BLOCK, C), 1, 2)
    kernel_t = jnp.swapaxes(kernel, 1, 2)
    inner_pairs = inner_map[0, 0, 0].reshape(-1)
    outer_pairs = outer_map[0, 0, 0].reshape(-1)
    inner_n = jnp.clip(inner_live[0, 0, 0], 0, PI).reshape(1)
    outer_n = jnp.clip(outer_live[0, 0, 0], 0, PB).reshape(1)
    received = received_blocks(local_grads, face_blocks[0, 0, 0])
    acc_in, acc_w = run_inner(inner_pairs, inner_n, local_grads, feats_t, kernel_t)
    input_grad, acc_w = run_outer(outer_pairs, outer_n, received, feats_t, kernel_t, acc_in, acc_w)
    bricks_all = lax.axis_size("gx") * lax.axis_size("gy") * lax.axis_size("gz")
    grad_scale = math.sqrt(27.0 / (bricks_all * PI * BLOCK))
    weight_grad = reduce_weights(acc_w, grad_scale)
    return (input_grad.reshape(1, 1, 1, NB * BLOCK, C), weight_grad)


def solution(mesh):
    in_specs = (
        P("gx", "gy", "gz", None, None),
        P("gx", "gy", "gz", None, None),
        P(),
        P("gx", "gy", "gz", None, None),
        P("gx", "gy", "gz", None, None),
        P("gx", "gy", "gz", None, None, None),
        P("gx", "gy", "gz"),
        P("gx", "gy", "gz"),
    )
    out_specs = (P("gx", "gy", "gz", None, None), P())
    return jax.shard_map(body, mesh=mesh, in_specs=in_specs, out_specs=out_specs, check_vma=False)
```

```python
import math

import jax
import jax.numpy as jnp
from jax import lax
from jax.experimental import pallas as pl
from jax.experimental.pallas import tpu as pltpu
from jax.sharding import PartitionSpec as P

C = 128
BLOCK = 128
NB = 32
PI = 288
PB = 32
UNROLL = 4


def extended(shard, sides, width):
    for axis, dim in sides:
        count, length = (lax.axis_size(axis), shard.shape[dim])
        up = [(i, (i + 1) % count) for i in range(count - 1)]
        down = [(j, i) for i, j in up]
        last = lax.slice_in_dim(shard, length - width, length, axis=dim)
        initial = lax.slice_in_dim(shard, 0, width, axis=dim)
        before = lax.ppermute(last, axis, up)
        after = lax.ppermute(initial, axis, down)
        shard = jnp.concatenate([before, shard, after], axis=dim)
    return shard


def received_blocks(local_grads, face_lists):
    got_x = extended(local_grads[face_lists[0]], (("gx", 0),), 1)
    got_y = extended(local_grads[face_lists[1]], (("gy", 0),), 1)
    got_z = extended(local_grads[face_lists[2]], (("gz", 0),), 1)
    return jnp.concatenate(
        [got_x[0], got_x[3], got_y[0], got_y[3], got_z[0], got_z[3]], axis=0
    )


def pair_loop(pairs_ref, live_ref, table_ref, table_base, update):
    def pair_ids(i):
        return (pairs_ref[3 * i], pairs_ref[3 * i + 1] - table_base, pairs_ref[3 * i + 2])

    def one_group(group, carry):
        ids = [pair_ids(group * UNROLL + j) for j in range(UNROLL)]
        grads = [table_ref[a] for _, a, _ in ids]
        update(ids, grads)
        return carry

    def one_pair(i, carry):
        k, a, b = pair_ids(i)
        update([(k, a, b)], [table_ref[a]])
        return carry

    live = live_ref[0]
    groups = live // UNROLL
    lax.fori_loop(0, groups, one_group, 0)
    lax.fori_loop(groups * UNROLL, live, one_pair, 0)


def weight_updater(ft_ref, acc_w):
    def update(ids, grads):
        terms = [
            jnp.dot(ft_ref[b], g, preferred_element_type=jnp.float32)
            for g, (_, _, b) in zip(grads, ids)
        ]
        for (k, _, _), term in zip(ids, terms):
            acc_w[k] += term

    return update


def input_updater(kt_ref, acc_in):
    def update(ids, grads):
        terms = [
            jnp.dot(g, kt_ref[k], preferred_element_type=jnp.float32)
            for g, (k, _, _) in zip(grads, ids)
        ]
        for (_, _, b), term in zip(ids, terms):
            acc_in[b] += term

    return update


def inner_weight_kernel(pairs_ref, live_ref, table_ref, ft_ref, acc_w):
    acc_w[...] = jnp.zeros_like(acc_w)
    pair_loop(pairs_ref, live_ref, table_ref, 0, weight_updater(ft_ref, acc_w))


def outer_weight_kernel(pairs_ref, live_ref, table_ref, ft_ref, w_start, acc_w):
    acc_w[...] = w_start[...]
    pair_loop(pairs_ref, live_ref, table_ref, NB, weight_updater(ft_ref, acc_w))


def input_kernel(inner_ref, inner_live_ref, outer_ref, outer_live_ref, local_ref, received_ref, kt_ref, after_ref, grad_out, acc_in):
    acc_in[...] = jnp.zeros_like(acc_in)
    update = input_updater(kt_ref, acc_in)
    pair_loop(inner_ref, inner_live_ref, local_ref, 0, update)
    pair_loop(outer_ref, outer_live_ref, received_ref, NB, update)
    grad_out[...] = acc_in[...].astype(grad_out.dtype)


def vmem():
    return pl.BlockSpec(memory_space=pltpu.MemorySpace.VMEM)


def smem():
    return pl.BlockSpec(memory_space=pltpu.MemorySpace.SMEM)


def cost(pairs):
    return pl.CostEstimate(
        flops=2 * pairs * BLOCK * C * C, transcendentals=0, bytes_accessed=6 * 1024 * 1024
    )


def run_inner_weights(pairs, live, table, ft):
    return pl.pallas_call(
        inner_weight_kernel,
        out_shape=jax.ShapeDtypeStruct((27, C, C), jnp.float32),
        in_specs=[smem(), smem(), vmem(), vmem()],
        out_specs=vmem(),
        cost_estimate=cost(PI),
        name="inner_weight_pairs",
    )(pairs, live, table, ft)


def run_outer_weights(pairs, live, table, ft, acc_w):
    return pl.pallas_call(
        outer_weight_kernel,
        out_shape=jax.ShapeDtypeStruct((27, C, C), jnp.float32),
        in_specs=[smem(), smem(), vmem(), vmem(), vmem()],
        out_specs=vmem(),
        input_output_aliases={4: 0},
        cost_estimate=cost(PB),
        name="outer_weight_pairs",
    )(pairs, live, table, ft, acc_w)


def run_inputs(inner_pairs, inner_n, outer_pairs, outer_n, local, received, kt, after):
    return pl.pallas_call(
        input_kernel,
        out_shape=jax.ShapeDtypeStruct((NB, BLOCK, C), jnp.bfloat16),
        in_specs=[smem(), smem(), smem(), smem(), vmem(), vmem(), vmem(), vmem()],
        out_specs=vmem(),
        scratch_shapes=[pltpu.VMEM((NB, BLOCK, C), jnp.float32)],
        cost_estimate=cost(PI + PB),
        name="input_pairs",
    )(inner_pairs, inner_n, outer_pairs, outer_n, local, received, kt, after)


def reduce_weights(weight_acc, grad_scale):
    flat = weight_acc.reshape(-1)
    for axis in ("gy", "gz", "gx"):
        n = lax.axis_size(axis)
        parts = lax.all_to_all(flat.reshape(n, -1), axis, 0, 0, tiled=True)
        flat = parts.reshape(n, -1).sum(axis=0)
    after = flat
    piece = (flat * grad_scale).astype(jnp.bfloat16)
    n = lax.axis_size("gx")
    copies = jnp.broadcast_to(piece[None], (n,) + piece.shape)
    piece = lax.all_to_all(copies, "gx", 0, 0, tiled=True).reshape(-1)
    piece = lax.all_gather(piece, "gz", tiled=True)
    piece = lax.all_gather(piece, "gy", tiled=True)
    return piece.reshape(weight_acc.shape), after


def body(features, output_grad, kernel, inner_map, outer_map, face_blocks, inner_live, outer_live):
    local_grads = output_grad[0, 0, 0].reshape(NB, BLOCK, C)
    feats_t = jnp.swapaxes(features[0, 0, 0].reshape(NB, BLOCK, C), 1, 2)
    kernel_t = jnp.swapaxes(kernel, 1, 2)
    inner_pairs = inner_map[0, 0, 0].reshape(-1)
    outer_pairs = outer_map[0, 0, 0].reshape(-1)
    inner_n = jnp.clip(inner_live[0, 0, 0], 0, PI).reshape(1)
    outer_n = jnp.clip(outer_live[0, 0, 0], 0, PB).reshape(1)
    received = received_blocks(local_grads, face_blocks[0, 0, 0])
    acc_w = run_inner_weights(inner_pairs, inner_n, local_grads, feats_t)
    acc_w = run_outer_weights(outer_pairs, outer_n, received, feats_t, acc_w)
    bricks_all = lax.axis_size("gx") * lax.axis_size("gy") * lax.axis_size("gz")
    grad_scale = math.sqrt(27.0 / (bricks_all * PI * BLOCK))
    weight_grad, after = reduce_weights(acc_w, grad_scale)
    input_grad = run_inputs(
        inner_pairs, inner_n, outer_pairs, outer_n, local_grads, received, kernel_t, after
    )
    return (input_grad.reshape(1, 1, 1, NB * BLOCK, C), weight_grad)


def solution(mesh):
    in_specs = (
        P("gx", "gy", "gz", None, None),
        P("gx", "gy", "gz", None, None),
        P(),
        P("gx", "gy", "gz", None, None),
        P("gx", "gy", "gz", None, None),
        P("gx", "gy", "gz", None, None, None),
        P("gx", "gy", "gz"),
        P("gx", "gy", "gz"),
    )
    out_specs = (P("gx", "gy", "gz", None, None), P())
    return jax.shard_map(body, mesh=mesh, in_specs=in_specs, out_specs=out_specs, check_vma=False)
```

```python
import math

import jax
import jax.numpy as jnp
from jax import lax
from jax.experimental import pallas as pl
from jax.experimental.pallas import tpu as pltpu
from jax.sharding import PartitionSpec as P

C = 128
BLOCK = 128
NB = 32
PI = 288
PB = 32
UNROLL = 4


def extended(shard, sides, width):
    for axis, dim in sides:
        count, length = (lax.axis_size(axis), shard.shape[dim])
        up = [(i, (i + 1) % count) for i in range(count - 1)]
        down = [(j, i) for i, j in up]
        last = lax.slice_in_dim(shard, length - width, length, axis=dim)
        initial = lax.slice_in_dim(shard, 0, width, axis=dim)
        before = lax.ppermute(last, axis, up)
        after = lax.ppermute(initial, axis, down)
        shard = jnp.concatenate([before, shard, after], axis=dim)
    return shard


def received_blocks(local_grads, face_lists):
    got_x = extended(local_grads[face_lists[0]], (("gx", 0),), 1)
    got_y = extended(local_grads[face_lists[1]], (("gy", 0),), 1)
    got_z = extended(local_grads[face_lists[2]], (("gz", 0),), 1)
    return jnp.concatenate(
        [got_x[0], got_x[3], got_y[0], got_y[3], got_z[0], got_z[3]], axis=0
    )


def pair_loop(pairs_ref, live_ref, table_ref, table_base, update):
    def pair_ids(i):
        return (pairs_ref[3 * i], pairs_ref[3 * i + 1] - table_base, pairs_ref[3 * i + 2])

    def one_group(group, carry):
        ids = [pair_ids(group * UNROLL + j) for j in range(UNROLL)]
        grads = [table_ref[a] for _, a, _ in ids]
        update(ids, grads)
        return carry

    def one_pair(i, carry):
        k, a, b = pair_ids(i)
        update([(k, a, b)], [table_ref[a]])
        return carry

    live = live_ref[0]
    groups = live // UNROLL
    lax.fori_loop(0, groups, one_group, 0)
    lax.fori_loop(groups * UNROLL, live, one_pair, 0)


def weight_updater(ft_ref, acc_w):
    def update(ids, grads):
        terms = [
            jnp.dot(ft_ref[b], g, preferred_element_type=jnp.float32)
            for g, (_, _, b) in zip(grads, ids)
        ]
        for (k, _, _), term in zip(ids, terms):
            acc_w[k] += term

    return update


def input_updater(kt_ref, acc_in):
    def update(ids, grads):
        terms = [
            jnp.dot(g, kt_ref[k], preferred_element_type=jnp.float32)
            for g, (k, _, _) in zip(grads, ids)
        ]
        for (_, _, b), term in zip(ids, terms):
            acc_in[b] += term

    return update


def inner_weight_kernel(pairs_ref, live_ref, table_ref, ft_ref, acc_w):
    acc_w[...] = jnp.zeros_like(acc_w)
    pair_loop(pairs_ref, live_ref, table_ref, 0, weight_updater(ft_ref, acc_w))


def outer_weight_kernel(pairs_ref, live_ref, table_ref, ft_ref, w_start, acc_w):
    acc_w[...] = w_start[...]
    pair_loop(pairs_ref, live_ref, table_ref, NB, weight_updater(ft_ref, acc_w))


def input_kernel(inner_ref, inner_live_ref, outer_ref, outer_live_ref, local_ref, received_ref, kt_ref, after_ref, grad_out, acc_in):
    acc_in[...] = jnp.zeros_like(acc_in)
    update = input_updater(kt_ref, acc_in)
    pair_loop(inner_ref, inner_live_ref, local_ref, 0, update)
    pair_loop(outer_ref, outer_live_ref, received_ref, NB, update)
    grad_out[...] = acc_in[...].astype(grad_out.dtype)


def vmem():
    return pl.BlockSpec(memory_space=pltpu.MemorySpace.VMEM)


def smem():
    return pl.BlockSpec(memory_space=pltpu.MemorySpace.SMEM)


def cost(pairs):
    return pl.CostEstimate(
        flops=2 * pairs * BLOCK * C * C, transcendentals=0, bytes_accessed=6 * 1024 * 1024
    )


def run_inner_weights(pairs, live, table, ft):
    return pl.pallas_call(
        inner_weight_kernel,
        out_shape=jax.ShapeDtypeStruct((27, C, C), jnp.float32),
        in_specs=[smem(), smem(), vmem(), vmem()],
        out_specs=vmem(),
        cost_estimate=cost(PI),
        name="inner_weight_pairs",
    )(pairs, live, table, ft)


def run_outer_weights(pairs, live, table, ft, acc_w):
    return pl.pallas_call(
        outer_weight_kernel,
        out_shape=jax.ShapeDtypeStruct((27, C, C), jnp.float32),
        in_specs=[smem(), smem(), vmem(), vmem(), vmem()],
        out_specs=vmem(),
        input_output_aliases={4: 0},
        cost_estimate=cost(PB),
        name="outer_weight_pairs",
    )(pairs, live, table, ft, acc_w)


def run_inputs(inner_pairs, inner_n, outer_pairs, outer_n, local, received, kt, after):
    return pl.pallas_call(
        input_kernel,
        out_shape=jax.ShapeDtypeStruct((NB, BLOCK, C), jnp.bfloat16),
        in_specs=[smem(), smem(), smem(), smem(), vmem(), vmem(), vmem(), vmem()],
        out_specs=vmem(),
        scratch_shapes=[pltpu.VMEM((NB, BLOCK, C), jnp.float32)],
        cost_estimate=cost(PI + PB),
        name="input_pairs",
    )(inner_pairs, inner_n, outer_pairs, outer_n, local, received, kt, after)


def reduce_weights(weight_acc, grad_scale):
    flat = weight_acc.reshape(-1)
    for axis in ("gy", "gz", "gx"):
        n = lax.axis_size(axis)
        parts = lax.all_to_all(flat.reshape(n, -1), axis, 0, 0, tiled=True)
        flat = parts.reshape(n, -1).sum(axis=0)
    after = flat
    piece = flat * grad_scale
    n = lax.axis_size("gx")
    copies = jnp.broadcast_to(piece[None], (n,) + piece.shape)
    piece = lax.all_to_all(copies, "gx", 0, 0, tiled=True).reshape(-1)
    piece = lax.optimization_barrier(lax.all_gather(piece, ("gy", "gz"), tiled=True))
    return piece.astype(jnp.bfloat16).reshape(weight_acc.shape), after


def body(features, output_grad, kernel, inner_map, outer_map, face_blocks, inner_live, outer_live):
    local_grads = output_grad[0, 0, 0].reshape(NB, BLOCK, C)
    feats_t = jnp.swapaxes(features[0, 0, 0].reshape(NB, BLOCK, C), 1, 2)
    kernel_t = jnp.swapaxes(kernel, 1, 2)
    inner_pairs = inner_map[0, 0, 0].reshape(-1)
    outer_pairs = outer_map[0, 0, 0].reshape(-1)
    inner_n = jnp.clip(inner_live[0, 0, 0], 0, PI).reshape(1)
    outer_n = jnp.clip(outer_live[0, 0, 0], 0, PB).reshape(1)
    received = received_blocks(local_grads, face_blocks[0, 0, 0])
    acc_w = run_inner_weights(inner_pairs, inner_n, local_grads, feats_t)
    acc_w = run_outer_weights(outer_pairs, outer_n, received, feats_t, acc_w)
    bricks_all = lax.axis_size("gx") * lax.axis_size("gy") * lax.axis_size("gz")
    grad_scale = math.sqrt(27.0 / (bricks_all * PI * BLOCK))
    weight_grad, after = reduce_weights(acc_w, grad_scale)
    input_grad = run_inputs(
        inner_pairs, inner_n, outer_pairs, outer_n, local_grads, received, kernel_t, after
    )
    return (input_grad.reshape(1, 1, 1, NB * BLOCK, C), weight_grad)


def solution(mesh):
    in_specs = (
        P("gx", "gy", "gz", None, None),
        P("gx", "gy", "gz", None, None),
        P(),
        P("gx", "gy", "gz", None, None),
        P("gx", "gy", "gz", None, None),
        P("gx", "gy", "gz", None, None, None),
        P("gx", "gy", "gz"),
        P("gx", "gy", "gz"),
    )
    out_specs = (P("gx", "gy", "gz", None, None), P())
    return jax.shard_map(body, mesh=mesh, in_specs=in_specs, out_specs=out_specs, check_vma=False)
```

```python
import math

import jax
import jax.numpy as jnp
from jax import lax
from jax.experimental import pallas as pl
from jax.experimental.pallas import tpu as pltpu
from jax.sharding import PartitionSpec as P

C = 128
BLOCK = 128
NB = 32
PI = 288
PB = 32
UNROLL = 4


def extended(shard, sides, width):
    for axis, dim in sides:
        count, length = (lax.axis_size(axis), shard.shape[dim])
        up = [(i, (i + 1) % count) for i in range(count - 1)]
        down = [(j, i) for i, j in up]
        last = lax.slice_in_dim(shard, length - width, length, axis=dim)
        initial = lax.slice_in_dim(shard, 0, width, axis=dim)
        before = lax.ppermute(last, axis, up)
        after = lax.ppermute(initial, axis, down)
        shard = jnp.concatenate([before, shard, after], axis=dim)
    return shard


def received_blocks(local_grads, face_lists):
    faces = local_grads[face_lists.reshape(-1)].reshape(3, 2, 4, BLOCK, C)
    got_x = extended(faces[0], (("gx", 0),), 1)
    got_y = extended(faces[1], (("gy", 0),), 1)
    got_z = extended(faces[2], (("gz", 0),), 1)
    return jnp.concatenate(
        [got_x[0], got_x[3], got_y[0], got_y[3], got_z[0], got_z[3]], axis=0
    )


def pair_loop(pairs_ref, live_ref, table_ref, table_base, update):
    def pair_ids(i):
        return (pairs_ref[i, 0], pairs_ref[i, 1] - table_base, pairs_ref[i, 2])

    def one_group(group, carry):
        ids = [pair_ids(group * UNROLL + j) for j in range(UNROLL)]
        grads = [table_ref[a] for _, a, _ in ids]
        update(ids, grads)
        return carry

    def one_pair(i, carry):
        k, a, b = pair_ids(i)
        update([(k, a, b)], [table_ref[a]])
        return carry

    live = jnp.clip(live_ref[0], 0, pairs_ref.shape[0])
    groups = live // UNROLL
    lax.fori_loop(0, groups, one_group, 0)
    lax.fori_loop(groups * UNROLL, live, one_pair, 0)


def weight_updater(ft_ref, acc_w):
    def update(ids, grads):
        terms = [
            jnp.dot(ft_ref[b], g, preferred_element_type=jnp.float32)
            for g, (_, _, b) in zip(grads, ids)
        ]
        for (k, _, _), term in zip(ids, terms):
            acc_w[k] += term

    return update


def input_updater(kt_ref, acc_in):
    def update(ids, grads):
        terms = [
            jnp.dot(g, kt_ref[k], preferred_element_type=jnp.float32)
            for g, (k, _, _) in zip(grads, ids)
        ]
        for (_, _, b), term in zip(ids, terms):
            acc_in[b] += term

    return update


def inner_weight_kernel(pairs_ref, live_ref, table_ref, ft_ref, acc_w):
    acc_w[...] = jnp.zeros_like(acc_w)
    pair_loop(pairs_ref, live_ref, table_ref, 0, weight_updater(ft_ref, acc_w))


def outer_weight_kernel(pairs_ref, live_ref, table_ref, ft_ref, w_start, acc_w):
    acc_w[...] = w_start[...]
    pair_loop(pairs_ref, live_ref, table_ref, NB, weight_updater(ft_ref, acc_w))


def input_kernel(inner_ref, inner_live_ref, outer_ref, outer_live_ref, local_ref, received_ref, kt_ref, after_ref, grad_out, acc_in):
    acc_in[...] = jnp.zeros_like(acc_in)
    update = input_updater(kt_ref, acc_in)
    pair_loop(inner_ref, inner_live_ref, local_ref, 0, update)
    pair_loop(outer_ref, outer_live_ref, received_ref, NB, update)
    grad_out[...] = acc_in[...].astype(grad_out.dtype)


def vmem():
    return pl.BlockSpec(memory_space=pltpu.MemorySpace.VMEM)


def smem():
    return pl.BlockSpec(memory_space=pltpu.MemorySpace.SMEM)


def cost(pairs):
    return pl.CostEstimate(
        flops=2 * pairs * BLOCK * C * C, transcendentals=0, bytes_accessed=6 * 1024 * 1024
    )


def run_inner_weights(pairs, live, table, ft):
    return pl.pallas_call(
        inner_weight_kernel,
        out_shape=jax.ShapeDtypeStruct((27, C, C), jnp.float32),
        in_specs=[smem(), smem(), vmem(), vmem()],
        out_specs=vmem(),
        cost_estimate=cost(PI),
        name="inner_weight_pairs",
    )(pairs, live, table, ft)


def run_outer_weights(pairs, live, table, ft, acc_w):
    return pl.pallas_call(
        outer_weight_kernel,
        out_shape=jax.ShapeDtypeStruct((27, C, C), jnp.float32),
        in_specs=[smem(), smem(), vmem(), vmem(), vmem()],
        out_specs=vmem(),
        input_output_aliases={4: 0},
        cost_estimate=cost(PB),
        name="outer_weight_pairs",
    )(pairs, live, table, ft, acc_w)


def run_inputs(inner_pairs, inner_n, outer_pairs, outer_n, local, received, kt, after):
    return pl.pallas_call(
        input_kernel,
        out_shape=jax.ShapeDtypeStruct((NB, BLOCK, C), jnp.bfloat16),
        in_specs=[smem(), smem(), smem(), smem(), vmem(), vmem(), vmem(), vmem()],
        out_specs=vmem(),
        scratch_shapes=[pltpu.VMEM((NB, BLOCK, C), jnp.float32)],
        cost_estimate=cost(PI + PB),
        name="input_pairs",
    )(inner_pairs, inner_n, outer_pairs, outer_n, local, received, kt, after)


def reduce_weights(weight_acc, grad_scale):
    flat = weight_acc.reshape(-1)
    for axis in ("gy", "gz", "gx"):
        n = lax.axis_size(axis)
        parts = lax.all_to_all(flat.reshape(n, -1), axis, 0, 0, tiled=True)
        flat = parts.reshape(n, -1).sum(axis=0)
    after = flat
    piece = (flat * grad_scale).astype(jnp.bfloat16)
    n = lax.axis_size("gx")
    copies = jnp.broadcast_to(piece[None], (n,) + piece.shape)
    piece = lax.all_to_all(copies, "gx", 0, 0, tiled=True).reshape(-1)
    piece = lax.all_gather(piece, "gz", tiled=True)
    piece = lax.all_gather(piece, "gy", tiled=True)
    return piece.reshape(weight_acc.shape), after


def body(features, output_grad, kernel, inner_map, outer_map, face_blocks, inner_live, outer_live):
    local_grads = output_grad[0, 0, 0].reshape(NB, BLOCK, C)
    feats_t = jnp.swapaxes(features[0, 0, 0].reshape(NB, BLOCK, C), 1, 2)
    kernel_t = jnp.swapaxes(kernel, 1, 2)
    inner_pairs = inner_map[0, 0, 0]
    outer_pairs = outer_map[0, 0, 0]
    inner_n = inner_live[0, 0]
    outer_n = outer_live[0, 0]
    received = received_blocks(local_grads, face_blocks[0, 0, 0])
    acc_w = run_inner_weights(inner_pairs, inner_n, local_grads, feats_t)
    acc_w = run_outer_weights(outer_pairs, outer_n, received, feats_t, acc_w)
    bricks_all = lax.axis_size("gx") * lax.axis_size("gy") * lax.axis_size("gz")
    grad_scale = math.sqrt(27.0 / (bricks_all * PI * BLOCK))
    weight_grad, after = reduce_weights(acc_w, grad_scale)
    input_grad = run_inputs(
        inner_pairs, inner_n, outer_pairs, outer_n, local_grads, received, kernel_t, after
    )
    return (input_grad.reshape(1, 1, 1, NB * BLOCK, C), weight_grad)


def solution(mesh):
    in_specs = (
        P("gx", "gy", "gz", None, None),
        P("gx", "gy", "gz", None, None),
        P(),
        P("gx", "gy", "gz", None, None),
        P("gx", "gy", "gz", None, None),
        P("gx", "gy", "gz", None, None, None),
        P("gx", "gy", "gz"),
        P("gx", "gy", "gz"),
    )
    out_specs = (P("gx", "gy", "gz", None, None), P())
    return jax.shard_map(body, mesh=mesh, in_specs=in_specs, out_specs=out_specs, check_vma=False)
```

```python
import math

import jax
import jax.numpy as jnp
from jax import lax
from jax.experimental import pallas as pl
from jax.experimental.pallas import tpu as pltpu
from jax.sharding import PartitionSpec as P

C = 128
BLOCK = 128
NB = 32
PI = 288
PB = 32
UNROLL = 8


def extended(shard, sides, width):
    for axis, dim in sides:
        count, length = (lax.axis_size(axis), shard.shape[dim])
        up = [(i, (i + 1) % count) for i in range(count - 1)]
        down = [(j, i) for i, j in up]
        last = lax.slice_in_dim(shard, length - width, length, axis=dim)
        initial = lax.slice_in_dim(shard, 0, width, axis=dim)
        before = lax.ppermute(last, axis, up)
        after = lax.ppermute(initial, axis, down)
        shard = jnp.concatenate([before, shard, after], axis=dim)
    return shard


def received_blocks(local_grads, face_lists):
    faces = local_grads[face_lists.reshape(-1)].reshape(3, 2, 4, BLOCK, C)
    got_x = extended(faces[0], (("gx", 0),), 1)
    got_y = extended(faces[1], (("gy", 0),), 1)
    got_z = extended(faces[2], (("gz", 0),), 1)
    return jnp.concatenate(
        [got_x[0], got_x[3], got_y[0], got_y[3], got_z[0], got_z[3]], axis=0
    )


def pair_loop(pairs_ref, live_ref, table_ref, table_base, update):
    def pair_ids(i):
        return (pairs_ref[i, 0], pairs_ref[i, 1] - table_base, pairs_ref[i, 2])

    def one_group(group, carry):
        ids = [pair_ids(group * UNROLL + j) for j in range(UNROLL)]
        grads = [table_ref[a] for _, a, _ in ids]
        update(ids, grads)
        return carry

    def one_pair(i, carry):
        k, a, b = pair_ids(i)
        update([(k, a, b)], [table_ref[a]])
        return carry

    live = jnp.clip(live_ref[0], 0, pairs_ref.shape[0])
    groups = live // UNROLL
    lax.fori_loop(0, groups, one_group, 0)
    lax.fori_loop(groups * UNROLL, live, one_pair, 0)


def weight_updater(ft_ref, acc_w):
    def update(ids, grads):
        terms = [
            jnp.dot(ft_ref[b], g, preferred_element_type=jnp.float32)
            for g, (_, _, b) in zip(grads, ids)
        ]
        for (k, _, _), term in zip(ids, terms):
            acc_w[k] += term

    return update


def input_updater(kt_ref, acc_in):
    def update(ids, grads):
        terms = [
            jnp.dot(g, kt_ref[k], preferred_element_type=jnp.float32)
            for g, (k, _, _) in zip(grads, ids)
        ]
        for (_, _, b), term in zip(ids, terms):
            acc_in[b] += term

    return update


def inner_weight_kernel(pairs_ref, live_ref, table_ref, ft_ref, acc_w):
    acc_w[...] = jnp.zeros_like(acc_w)
    pair_loop(pairs_ref, live_ref, table_ref, 0, weight_updater(ft_ref, acc_w))


def outer_weight_kernel(pairs_ref, live_ref, table_ref, ft_ref, w_start, acc_w):
    acc_w[...] = w_start[...]
    pair_loop(pairs_ref, live_ref, table_ref, NB, weight_updater(ft_ref, acc_w))


def input_kernel(inner_ref, inner_live_ref, outer_ref, outer_live_ref, local_ref, received_ref, kt_ref, after_ref, grad_out, acc_in):
    acc_in[...] = jnp.zeros_like(acc_in)
    update = input_updater(kt_ref, acc_in)
    pair_loop(inner_ref, inner_live_ref, local_ref, 0, update)
    pair_loop(outer_ref, outer_live_ref, received_ref, NB, update)
    grad_out[...] = acc_in[...].astype(grad_out.dtype)


def vmem():
    return pl.BlockSpec(memory_space=pltpu.MemorySpace.VMEM)


def smem():
    return pl.BlockSpec(memory_space=pltpu.MemorySpace.SMEM)


def cost(pairs):
    return pl.CostEstimate(
        flops=2 * pairs * BLOCK * C * C, transcendentals=0, bytes_accessed=6 * 1024 * 1024
    )


def run_inner_weights(pairs, live, table, ft):
    return pl.pallas_call(
        inner_weight_kernel,
        out_shape=jax.ShapeDtypeStruct((27, C, C), jnp.float32),
        in_specs=[smem(), smem(), vmem(), vmem()],
        out_specs=vmem(),
        cost_estimate=cost(PI),
        name="inner_weight_pairs",
    )(pairs, live, table, ft)


def run_outer_weights(pairs, live, table, ft, acc_w):
    return pl.pallas_call(
        outer_weight_kernel,
        out_shape=jax.ShapeDtypeStruct((27, C, C), jnp.float32),
        in_specs=[smem(), smem(), vmem(), vmem(), vmem()],
        out_specs=vmem(),
        input_output_aliases={4: 0},
        cost_estimate=cost(PB),
        name="outer_weight_pairs",
    )(pairs, live, table, ft, acc_w)


def run_inputs(inner_pairs, inner_n, outer_pairs, outer_n, local, received, kt, after):
    return pl.pallas_call(
        input_kernel,
        out_shape=jax.ShapeDtypeStruct((NB, BLOCK, C), jnp.bfloat16),
        in_specs=[smem(), smem(), smem(), smem(), vmem(), vmem(), vmem(), vmem()],
        out_specs=vmem(),
        scratch_shapes=[pltpu.VMEM((NB, BLOCK, C), jnp.float32)],
        cost_estimate=cost(PI + PB),
        name="input_pairs",
    )(inner_pairs, inner_n, outer_pairs, outer_n, local, received, kt, after)


def reduce_weights(weight_acc, grad_scale):
    flat = weight_acc.reshape(-1)
    for axis in ("gy", "gz", "gx"):
        n = lax.axis_size(axis)
        parts = lax.all_to_all(flat.reshape(n, -1), axis, 0, 0, tiled=True)
        flat = parts.reshape(n, -1).sum(axis=0)
    after = flat
    piece = (flat * grad_scale).astype(jnp.bfloat16)
    n = lax.axis_size("gx")
    copies = jnp.broadcast_to(piece[None], (n,) + piece.shape)
    piece = lax.all_to_all(copies, "gx", 0, 0, tiled=True).reshape(-1)
    piece = lax.all_gather(piece, "gz", tiled=True)
    piece = lax.all_gather(piece, "gy", tiled=True)
    return piece.reshape(weight_acc.shape), after


def body(features, output_grad, kernel, inner_map, outer_map, face_blocks, inner_live, outer_live):
    local_grads = output_grad[0, 0, 0].reshape(NB, BLOCK, C)
    feats_t = jnp.swapaxes(features[0, 0, 0].reshape(NB, BLOCK, C), 1, 2)
    kernel_t = jnp.swapaxes(kernel, 1, 2)
    inner_pairs = inner_map[0, 0, 0]
    outer_pairs = outer_map[0, 0, 0]
    inner_n = inner_live[0, 0]
    outer_n = outer_live[0, 0]
    received = received_blocks(local_grads, face_blocks[0, 0, 0])
    acc_w = run_inner_weights(inner_pairs, inner_n, local_grads, feats_t)
    acc_w = run_outer_weights(outer_pairs, outer_n, received, feats_t, acc_w)
    bricks_all = lax.axis_size("gx") * lax.axis_size("gy") * lax.axis_size("gz")
    grad_scale = math.sqrt(27.0 / (bricks_all * PI * BLOCK))
    weight_grad, after = reduce_weights(acc_w, grad_scale)
    input_grad = run_inputs(
        inner_pairs, inner_n, outer_pairs, outer_n, local_grads, received, kernel_t, after
    )
    return (input_grad.reshape(1, 1, 1, NB * BLOCK, C), weight_grad)


def solution(mesh):
    in_specs = (
        P("gx", "gy", "gz", None, None),
        P("gx", "gy", "gz", None, None),
        P(),
        P("gx", "gy", "gz", None, None),
        P("gx", "gy", "gz", None, None),
        P("gx", "gy", "gz", None, None, None),
        P("gx", "gy", "gz"),
        P("gx", "gy", "gz"),
    )
    out_specs = (P("gx", "gy", "gz", None, None), P())
    return jax.shard_map(body, mesh=mesh, in_specs=in_specs, out_specs=out_specs, check_vma=False)
```

```python
import math

import jax
import jax.numpy as jnp
from jax import lax
from jax.experimental import pallas as pl
from jax.experimental.pallas import tpu as pltpu
from jax.sharding import PartitionSpec as P

C = 128
BLOCK = 128
NB = 32
PI = 288
PB = 32
UNROLL = 16


def extended(shard, sides, width):
    for axis, dim in sides:
        count, length = (lax.axis_size(axis), shard.shape[dim])
        up = [(i, (i + 1) % count) for i in range(count - 1)]
        down = [(j, i) for i, j in up]
        last = lax.slice_in_dim(shard, length - width, length, axis=dim)
        initial = lax.slice_in_dim(shard, 0, width, axis=dim)
        before = lax.ppermute(last, axis, up)
        after = lax.ppermute(initial, axis, down)
        shard = jnp.concatenate([before, shard, after], axis=dim)
    return shard


def received_blocks(local_grads, face_lists):
    faces = local_grads[face_lists.reshape(-1)].reshape(3, 2, 4, BLOCK, C)
    got_x = extended(faces[0], (("gx", 0),), 1)
    got_y = extended(faces[1], (("gy", 0),), 1)
    got_z = extended(faces[2], (("gz", 0),), 1)
    return jnp.concatenate(
        [got_x[0], got_x[3], got_y[0], got_y[3], got_z[0], got_z[3]], axis=0
    )


def pair_loop(pairs_ref, live_ref, table_ref, table_base, update):
    def pair_ids(i):
        return (pairs_ref[i, 0], pairs_ref[i, 1] - table_base, pairs_ref[i, 2])

    def one_group(group, carry):
        ids = [pair_ids(group * UNROLL + j) for j in range(UNROLL)]
        grads = [table_ref[a] for _, a, _ in ids]
        update(ids, grads)
        return carry

    def one_pair(i, carry):
        k, a, b = pair_ids(i)
        update([(k, a, b)], [table_ref[a]])
        return carry

    live = jnp.clip(live_ref[0], 0, pairs_ref.shape[0])
    groups = live // UNROLL
    lax.fori_loop(0, groups, one_group, 0)
    lax.fori_loop(groups * UNROLL, live, one_pair, 0)


def weight_updater(ft_ref, acc_w):
    def update(ids, grads):
        terms = [
            jnp.dot(ft_ref[b], g, preferred_element_type=jnp.float32)
            for g, (_, _, b) in zip(grads, ids)
        ]
        for (k, _, _), term in zip(ids, terms):
            acc_w[k] += term

    return update


def input_updater(kt_ref, acc_in):
    def update(ids, grads):
        terms = [
            jnp.dot(g, kt_ref[k], preferred_element_type=jnp.float32)
            for g, (k, _, _) in zip(grads, ids)
        ]
        for (_, _, b), term in zip(ids, terms):
            acc_in[b] += term

    return update


def inner_weight_kernel(pairs_ref, live_ref, table_ref, ft_ref, acc_w):
    acc_w[...] = jnp.zeros_like(acc_w)
    pair_loop(pairs_ref, live_ref, table_ref, 0, weight_updater(ft_ref, acc_w))


def outer_weight_kernel(pairs_ref, live_ref, table_ref, ft_ref, w_start, acc_w):
    acc_w[...] = w_start[...]
    pair_loop(pairs_ref, live_ref, table_ref, NB, weight_updater(ft_ref, acc_w))


def input_kernel(inner_ref, inner_live_ref, outer_ref, outer_live_ref, local_ref, received_ref, kt_ref, after_ref, grad_out, acc_in):
    acc_in[...] = jnp.zeros_like(acc_in)
    update = input_updater(kt_ref, acc_in)
    pair_loop(inner_ref, inner_live_ref, local_ref, 0, update)
    pair_loop(outer_ref, outer_live_ref, received_ref, NB, update)
    grad_out[...] = acc_in[...].astype(grad_out.dtype)


def vmem():
    return pl.BlockSpec(memory_space=pltpu.MemorySpace.VMEM)


def smem():
    return pl.BlockSpec(memory_space=pltpu.MemorySpace.SMEM)


def cost(pairs):
    return pl.CostEstimate(
        flops=2 * pairs * BLOCK * C * C, transcendentals=0, bytes_accessed=6 * 1024 * 1024
    )


def run_inner_weights(pairs, live, table, ft):
    return pl.pallas_call(
        inner_weight_kernel,
        out_shape=jax.ShapeDtypeStruct((27, C, C), jnp.float32),
        in_specs=[smem(), smem(), vmem(), vmem()],
        out_specs=vmem(),
        cost_estimate=cost(PI),
        name="inner_weight_pairs",
    )(pairs, live, table, ft)


def run_outer_weights(pairs, live, table, ft, acc_w):
    return pl.pallas_call(
        outer_weight_kernel,
        out_shape=jax.ShapeDtypeStruct((27, C, C), jnp.float32),
        in_specs=[smem(), smem(), vmem(), vmem(), vmem()],
        out_specs=vmem(),
        input_output_aliases={4: 0},
        cost_estimate=cost(PB),
        name="outer_weight_pairs",
    )(pairs, live, table, ft, acc_w)


def run_inputs(inner_pairs, inner_n, outer_pairs, outer_n, local, received, kt, after):
    return pl.pallas_call(
        input_kernel,
        out_shape=jax.ShapeDtypeStruct((NB, BLOCK, C), jnp.bfloat16),
        in_specs=[smem(), smem(), smem(), smem(), vmem(), vmem(), vmem(), vmem()],
        out_specs=vmem(),
        scratch_shapes=[pltpu.VMEM((NB, BLOCK, C), jnp.float32)],
        cost_estimate=cost(PI + PB),
        name="input_pairs",
    )(inner_pairs, inner_n, outer_pairs, outer_n, local, received, kt, after)


def reduce_weights(weight_acc, grad_scale):
    flat = weight_acc.reshape(-1)
    for axis in ("gy", "gz", "gx"):
        n = lax.axis_size(axis)
        parts = lax.all_to_all(flat.reshape(n, -1), axis, 0, 0, tiled=True)
        flat = parts.reshape(n, -1).sum(axis=0)
    after = flat
    piece = (flat * grad_scale).astype(jnp.bfloat16)
    n = lax.axis_size("gx")
    copies = jnp.broadcast_to(piece[None], (n,) + piece.shape)
    piece = lax.all_to_all(copies, "gx", 0, 0, tiled=True).reshape(-1)
    piece = lax.all_gather(piece, "gz", tiled=True)
    piece = lax.all_gather(piece, "gy", tiled=True)
    return piece.reshape(weight_acc.shape), after


def body(features, output_grad, kernel, inner_map, outer_map, face_blocks, inner_live, outer_live):
    local_grads = output_grad[0, 0, 0].reshape(NB, BLOCK, C)
    feats_t = jnp.swapaxes(features[0, 0, 0].reshape(NB, BLOCK, C), 1, 2)
    kernel_t = jnp.swapaxes(kernel, 1, 2)
    inner_pairs = inner_map[0, 0, 0]
    outer_pairs = outer_map[0, 0, 0]
    inner_n = inner_live[0, 0]
    outer_n = outer_live[0, 0]
    received = received_blocks(local_grads, face_blocks[0, 0, 0])
    acc_w = run_inner_weights(inner_pairs, inner_n, local_grads, feats_t)
    acc_w = run_outer_weights(outer_pairs, outer_n, received, feats_t, acc_w)
    bricks_all = lax.axis_size("gx") * lax.axis_size("gy") * lax.axis_size("gz")
    grad_scale = math.sqrt(27.0 / (bricks_all * PI * BLOCK))
    weight_grad, after = reduce_weights(acc_w, grad_scale)
    input_grad = run_inputs(
        inner_pairs, inner_n, outer_pairs, outer_n, local_grads, received, kernel_t, after
    )
    return (input_grad.reshape(1, 1, 1, NB * BLOCK, C), weight_grad)


def solution(mesh):
    in_specs = (
        P("gx", "gy", "gz", None, None),
        P("gx", "gy", "gz", None, None),
        P(),
        P("gx", "gy", "gz", None, None),
        P("gx", "gy", "gz", None, None),
        P("gx", "gy", "gz", None, None, None),
        P("gx", "gy", "gz"),
        P("gx", "gy", "gz"),
    )
    out_specs = (P("gx", "gy", "gz", None, None), P())
    return jax.shard_map(body, mesh=mesh, in_specs=in_specs, out_specs=out_specs, check_vma=False)
```

```python
import math

import jax
import jax.numpy as jnp
from jax import lax
from jax.experimental import pallas as pl
from jax.experimental.pallas import tpu as pltpu
from jax.sharding import PartitionSpec as P

C = 128
BLOCK = 128
NB = 32
PI = 288
PB = 32
UNROLL = 16


def extended(shard, sides, width):
    for axis, dim in sides:
        count, length = (lax.axis_size(axis), shard.shape[dim])
        up = [(i, (i + 1) % count) for i in range(count - 1)]
        down = [(j, i) for i, j in up]
        last = lax.slice_in_dim(shard, length - width, length, axis=dim)
        initial = lax.slice_in_dim(shard, 0, width, axis=dim)
        before = lax.ppermute(last, axis, up)
        after = lax.ppermute(initial, axis, down)
        shard = jnp.concatenate([before, shard, after], axis=dim)
    return shard


def received_blocks(local_grads, face_lists):
    faces = local_grads[face_lists.reshape(-1)].reshape(3, 2, 4, BLOCK, C)
    got_x = extended(faces[0], (("gx", 0),), 1)
    got_y = extended(faces[1], (("gy", 0),), 1)
    got_z = extended(faces[2], (("gz", 0),), 1)
    return jnp.concatenate(
        [got_x[0], got_x[3], got_y[0], got_y[3], got_z[0], got_z[3]], axis=0
    )


def pair_loop(pairs_ref, live_ref, table_ref, table_base, update):
    def pair_ids(i):
        return (pairs_ref[i, 0], pairs_ref[i, 1] - table_base, pairs_ref[i, 2])

    def one_group(group, carry):
        ids = [pair_ids(group * UNROLL + j) for j in range(UNROLL)]
        grads = [table_ref[a] for _, a, _ in ids]
        update(ids, grads)
        return carry

    def one_pair(i, carry):
        k, a, b = pair_ids(i)
        update([(k, a, b)], [table_ref[a]])
        return carry

    live = jnp.clip(live_ref[0], 0, pairs_ref.shape[0])
    groups = live // UNROLL
    lax.fori_loop(0, groups, one_group, 0)
    lax.fori_loop(groups * UNROLL, live, one_pair, 0)


def weight_updater(ft_ref, acc_w):
    def update(ids, grads):
        terms = [
            jnp.dot(ft_ref[b], g, preferred_element_type=jnp.float32)
            for g, (_, _, b) in zip(grads, ids)
        ]
        for (k, _, _), term in zip(ids, terms):
            acc_w[k] += term

    return update


def input_updater(kt_ref, acc_in):
    def update(ids, grads):
        terms = [
            jnp.dot(g, kt_ref[k], preferred_element_type=jnp.float32)
            for g, (k, _, _) in zip(grads, ids)
        ]
        for (_, _, b), term in zip(ids, terms):
            acc_in[b] += term

    return update


def weight_kernel(inner_ref, inner_live_ref, outer_ref, outer_live_ref, local_ref, received_ref, ft_ref, acc_w):
    acc_w[...] = jnp.zeros_like(acc_w)
    update = weight_updater(ft_ref, acc_w)
    pair_loop(inner_ref, inner_live_ref, local_ref, 0, update)
    pair_loop(outer_ref, outer_live_ref, received_ref, NB, update)


def input_kernel(inner_ref, inner_live_ref, outer_ref, outer_live_ref, local_ref, received_ref, kt_ref, after_ref, grad_out, acc_in):
    acc_in[...] = jnp.zeros_like(acc_in)
    update = input_updater(kt_ref, acc_in)
    pair_loop(inner_ref, inner_live_ref, local_ref, 0, update)
    pair_loop(outer_ref, outer_live_ref, received_ref, NB, update)
    grad_out[...] = acc_in[...].astype(grad_out.dtype)


def vmem():
    return pl.BlockSpec(memory_space=pltpu.MemorySpace.VMEM)


def smem():
    return pl.BlockSpec(memory_space=pltpu.MemorySpace.SMEM)


def cost(pairs):
    return pl.CostEstimate(
        flops=2 * pairs * BLOCK * C * C, transcendentals=0, bytes_accessed=6 * 1024 * 1024
    )


def run_weights(inner_pairs, inner_n, outer_pairs, outer_n, local, received, ft):
    return pl.pallas_call(
        weight_kernel,
        out_shape=jax.ShapeDtypeStruct((27, C, C), jnp.float32),
        in_specs=[smem(), smem(), smem(), smem(), vmem(), vmem(), vmem()],
        out_specs=vmem(),
        cost_estimate=cost(PI + PB),
        name="weight_pairs",
    )(inner_pairs, inner_n, outer_pairs, outer_n, local, received, ft)


def run_inputs(inner_pairs, inner_n, outer_pairs, outer_n, local, received, kt, after):
    return pl.pallas_call(
        input_kernel,
        out_shape=jax.ShapeDtypeStruct((NB, BLOCK, C), jnp.bfloat16),
        in_specs=[smem(), smem(), smem(), smem(), vmem(), vmem(), vmem(), vmem()],
        out_specs=vmem(),
        scratch_shapes=[pltpu.VMEM((NB, BLOCK, C), jnp.float32)],
        cost_estimate=cost(PI + PB),
        name="input_pairs",
    )(inner_pairs, inner_n, outer_pairs, outer_n, local, received, kt, after)


def reduce_weights(weight_acc, grad_scale):
    flat = weight_acc.reshape(-1)
    for axis in ("gy", "gz", "gx"):
        n = lax.axis_size(axis)
        parts = lax.all_to_all(flat.reshape(n, -1), axis, 0, 0, tiled=True)
        flat = parts.reshape(n, -1).sum(axis=0)
    after = flat
    piece = (flat * grad_scale).astype(jnp.bfloat16)
    n = lax.axis_size("gx")
    copies = jnp.broadcast_to(piece[None], (n,) + piece.shape)
    piece = lax.all_to_all(copies, "gx", 0, 0, tiled=True).reshape(-1)
    piece = lax.all_gather(piece, "gz", tiled=True)
    piece = lax.all_gather(piece, "gy", tiled=True)
    return piece.reshape(weight_acc.shape), after


def body(features, output_grad, kernel, inner_map, outer_map, face_blocks, inner_live, outer_live):
    local_grads = output_grad[0, 0, 0].reshape(NB, BLOCK, C)
    feats_t = jnp.swapaxes(features[0, 0, 0].reshape(NB, BLOCK, C), 1, 2)
    kernel_t = jnp.swapaxes(kernel, 1, 2)
    inner_pairs = inner_map[0, 0, 0]
    outer_pairs = outer_map[0, 0, 0]
    inner_n = inner_live[0, 0]
    outer_n = outer_live[0, 0]
    received = received_blocks(local_grads, face_blocks[0, 0, 0])
    acc_w = run_weights(inner_pairs, inner_n, outer_pairs, outer_n, local_grads, received, feats_t)
    bricks_all = lax.axis_size("gx") * lax.axis_size("gy") * lax.axis_size("gz")
    grad_scale = math.sqrt(27.0 / (bricks_all * PI * BLOCK))
    weight_grad, after = reduce_weights(acc_w, grad_scale)
    input_grad = run_inputs(
        inner_pairs, inner_n, outer_pairs, outer_n, local_grads, received, kernel_t, after
    )
    return (input_grad.reshape(1, 1, 1, NB * BLOCK, C), weight_grad)


def solution(mesh):
    in_specs = (
        P("gx", "gy", "gz", None, None),
        P("gx", "gy", "gz", None, None),
        P(),
        P("gx", "gy", "gz", None, None),
        P("gx", "gy", "gz", None, None),
        P("gx", "gy", "gz", None, None, None),
        P("gx", "gy", "gz"),
        P("gx", "gy", "gz"),
    )
    out_specs = (P("gx", "gy", "gz", None, None), P())
    return jax.shard_map(body, mesh=mesh, in_specs=in_specs, out_specs=out_specs, check_vma=False)
```

```python
import math

import jax
import jax.numpy as jnp
from jax import lax
from jax.experimental import pallas as pl
from jax.experimental.pallas import tpu as pltpu
from jax.sharding import Mesh
from jax.sharding import PartitionSpec as P

C = 128
BLOCK = 128
NB = 32
PI = 288
PB = 32
UNROLL = 16
GX = ("zh", "x")
GY = ("y", "c")
ZZ = ("zh", "gz")


def extended(shard, sides, width):
    for axis, dim in sides:
        count, length = (lax.axis_size(axis), shard.shape[dim])
        up = [(i, (i + 1) % count) for i in range(count - 1)]
        down = [(j, i) for i, j in up]
        last = lax.slice_in_dim(shard, length - width, length, axis=dim)
        initial = lax.slice_in_dim(shard, 0, width, axis=dim)
        before = lax.ppermute(last, axis, up)
        after = lax.ppermute(initial, axis, down)
        shard = jnp.concatenate([before, shard, after], axis=dim)
    return shard


def received_blocks(local_grads, face_lists):
    faces = local_grads[face_lists.reshape(-1)].reshape(3, 2, 4, BLOCK, C)
    got_x = extended(faces[0], ((GX, 0),), 1)
    got_y = extended(faces[1], ((GY, 0),), 1)
    got_z = extended(faces[2], (("gz", 0),), 1)
    return jnp.concatenate(
        [got_x[0], got_x[3], got_y[0], got_y[3], got_z[0], got_z[3]], axis=0
    )


def pair_loop(pairs_ref, live_ref, table_ref, table_base, update):
    def pair_ids(i):
        return (pairs_ref[i, 0], pairs_ref[i, 1] - table_base, pairs_ref[i, 2])

    def one_group(group, carry):
        ids = [pair_ids(group * UNROLL + j) for j in range(UNROLL)]
        grads = [table_ref[a] for _, a, _ in ids]
        update(ids, grads)
        return carry

    def one_pair(i, carry):
        k, a, b = pair_ids(i)
        update([(k, a, b)], [table_ref[a]])
        return carry

    live = jnp.clip(live_ref[0], 0, pairs_ref.shape[0])
    groups = live // UNROLL
    lax.fori_loop(0, groups, one_group, 0)
    lax.fori_loop(groups * UNROLL, live, one_pair, 0)


def weight_updater(ft_ref, acc_w):
    def update(ids, grads):
        terms = [
            jnp.dot(ft_ref[b], g, preferred_element_type=jnp.float32)
            for g, (_, _, b) in zip(grads, ids)
        ]
        for (k, _, _), term in zip(ids, terms):
            acc_w[k] += term

    return update


def input_updater(kt_ref, acc_in):
    def update(ids, grads):
        terms = [
            jnp.dot(g, kt_ref[k], preferred_element_type=jnp.float32)
            for g, (k, _, _) in zip(grads, ids)
        ]
        for (_, _, b), term in zip(ids, terms):
            acc_in[b] += term

    return update


def weight_kernel(inner_ref, inner_live_ref, outer_ref, outer_live_ref, local_ref, received_ref, ft_ref, acc_w):
    acc_w[...] = jnp.zeros_like(acc_w)
    update = weight_updater(ft_ref, acc_w)
    pair_loop(inner_ref, inner_live_ref, local_ref, 0, update)
    pair_loop(outer_ref, outer_live_ref, received_ref, NB, update)


def input_kernel(inner_ref, inner_live_ref, outer_ref, outer_live_ref, local_ref, received_ref, kt_ref, after_ref, grad_out, acc_in):
    acc_in[...] = jnp.zeros_like(acc_in)
    update = input_updater(kt_ref, acc_in)
    pair_loop(inner_ref, inner_live_ref, local_ref, 0, update)
    pair_loop(outer_ref, outer_live_ref, received_ref, NB, update)
    grad_out[...] = acc_in[...].astype(grad_out.dtype)


def vmem():
    return pl.BlockSpec(memory_space=pltpu.MemorySpace.VMEM)


def smem():
    return pl.BlockSpec(memory_space=pltpu.MemorySpace.SMEM)


def cost(pairs):
    return pl.CostEstimate(
        flops=2 * pairs * BLOCK * C * C, transcendentals=0, bytes_accessed=6 * 1024 * 1024
    )


def run_weights(inner_pairs, inner_n, outer_pairs, outer_n, local, received, ft):
    return pl.pallas_call(
        weight_kernel,
        out_shape=jax.ShapeDtypeStruct((27, C, C), jnp.float32),
        in_specs=[smem(), smem(), smem(), smem(), vmem(), vmem(), vmem()],
        out_specs=vmem(),
        cost_estimate=cost(PI + PB),
        name="weight_pairs",
    )(inner_pairs, inner_n, outer_pairs, outer_n, local, received, ft)


def run_inputs(inner_pairs, inner_n, outer_pairs, outer_n, local, received, kt, after):
    return pl.pallas_call(
        input_kernel,
        out_shape=jax.ShapeDtypeStruct((NB, BLOCK, C), jnp.bfloat16),
        in_specs=[smem(), smem(), smem(), smem(), vmem(), vmem(), vmem(), vmem()],
        out_specs=vmem(),
        scratch_shapes=[pltpu.VMEM((NB, BLOCK, C), jnp.float32)],
        cost_estimate=cost(PI + PB),
        name="input_pairs",
    )(inner_pairs, inner_n, outer_pairs, outer_n, local, received, kt, after)


def reduce_weights(weight_acc, grad_scale):
    flat = weight_acc.reshape(-1)
    for axis in (GY, "x", ZZ):
        n = lax.axis_size(axis)
        parts = lax.all_to_all(flat.reshape(n, -1), axis, 0, 0, tiled=True)
        flat = parts.reshape(n, -1).sum(axis=0)
    after = flat
    piece = (flat * grad_scale).astype(jnp.bfloat16)
    n = lax.axis_size(ZZ)
    copies = jnp.broadcast_to(piece[None], (n,) + piece.shape)
    piece = lax.all_to_all(copies, ZZ, 0, 0, tiled=True).reshape(-1)
    piece = lax.all_gather(piece, "x", tiled=True)
    piece = lax.all_gather(piece, GY, tiled=True)
    return piece.reshape(weight_acc.shape), after


def body(features, output_grad, kernel, inner_map, outer_map, face_blocks, inner_live, outer_live):
    local_grads = output_grad[0, 0, 0].reshape(NB, BLOCK, C)
    feats_t = jnp.swapaxes(features[0, 0, 0].reshape(NB, BLOCK, C), 1, 2)
    kernel_t = jnp.swapaxes(kernel, 1, 2)
    inner_pairs = inner_map[0, 0, 0]
    outer_pairs = outer_map[0, 0, 0]
    inner_n = inner_live[0, 0]
    outer_n = outer_live[0, 0]
    received = received_blocks(local_grads, face_blocks[0, 0, 0])
    acc_w = run_weights(inner_pairs, inner_n, outer_pairs, outer_n, local_grads, received, feats_t)
    bricks_all = lax.axis_size(GX) * lax.axis_size(GY) * lax.axis_size("gz")
    grad_scale = math.sqrt(27.0 / (bricks_all * PI * BLOCK))
    weight_grad, after = reduce_weights(acc_w, grad_scale)
    input_grad = run_inputs(
        inner_pairs, inner_n, outer_pairs, outer_n, local_grads, received, kernel_t, after
    )
    return (input_grad.reshape(1, 1, 1, NB * BLOCK, C), weight_grad)


def solution(mesh):
    gx, gy, gz = (mesh.shape[name] for name in ("gx", "gy", "gz"))
    along_x = len({device.coords[0] for device in mesh.devices.flat})
    cores = gy // len({device.coords[1] for device in mesh.devices.flat})
    fine = Mesh(
        mesh.devices.reshape(gx // along_x, along_x, gy // cores, cores, gz),
        ("zh", "x", "y", "c", "gz"),
    )
    brick = P(GX, GY, "gz", None, None)
    in_specs = (
        brick,
        brick,
        P(),
        brick,
        brick,
        P(GX, GY, "gz", None, None, None),
        P(GX, GY, "gz"),
        P(GX, GY, "gz"),
    )
    out_specs = (brick, P())
    return jax.shard_map(body, mesh=fine, in_specs=in_specs, out_specs=out_specs, check_vma=False)
```

```python
import math

import jax
import jax.numpy as jnp
from jax import lax
from jax.experimental import pallas as pl
from jax.experimental.pallas import tpu as pltpu
from jax.sharding import Mesh
from jax.sharding import PartitionSpec as P

C = 128
BLOCK = 128
NB = 32
PI = 288
PB = 32
UNROLL = 32
GX = ("zh", "x")
GY = ("y", "c")
ZZ = ("zh", "gz")


def extended(shard, sides, width):
    for axis, dim in sides:
        count, length = (lax.axis_size(axis), shard.shape[dim])
        up = [(i, (i + 1) % count) for i in range(count - 1)]
        down = [(j, i) for i, j in up]
        last = lax.slice_in_dim(shard, length - width, length, axis=dim)
        initial = lax.slice_in_dim(shard, 0, width, axis=dim)
        before = lax.ppermute(last, axis, up)
        after = lax.ppermute(initial, axis, down)
        shard = jnp.concatenate([before, shard, after], axis=dim)
    return shard


def received_blocks(local_grads, face_lists):
    faces = local_grads[face_lists.reshape(-1)].reshape(3, 2, 4, BLOCK, C)
    got_x = extended(faces[0], ((GX, 0),), 1)
    got_y = extended(faces[1], ((GY, 0),), 1)
    got_z = extended(faces[2], (("gz", 0),), 1)
    return jnp.concatenate(
        [got_x[0], got_x[3], got_y[0], got_y[3], got_z[0], got_z[3]], axis=0
    )


def pair_loop(pairs_ref, live_ref, table_ref, table_base, update):
    def pair_ids(i):
        return (pairs_ref[i, 0], pairs_ref[i, 1] - table_base, pairs_ref[i, 2])

    def one_group(group, carry):
        ids = [pair_ids(group * UNROLL + j) for j in range(UNROLL)]
        grads = [table_ref[a] for _, a, _ in ids]
        update(ids, grads)
        return carry

    def one_pair(i, carry):
        k, a, b = pair_ids(i)
        update([(k, a, b)], [table_ref[a]])
        return carry

    live = jnp.clip(live_ref[0], 0, pairs_ref.shape[0])
    groups = live // UNROLL
    lax.fori_loop(0, groups, one_group, 0)
    lax.fori_loop(groups * UNROLL, live, one_pair, 0)


def weight_updater(ft_ref, acc_w):
    def update(ids, grads):
        terms = [
            jnp.dot(ft_ref[b], g, preferred_element_type=jnp.float32)
            for g, (_, _, b) in zip(grads, ids)
        ]
        for (k, _, _), term in zip(ids, terms):
            acc_w[k] += term

    return update


def input_updater(kt_ref, acc_in):
    def update(ids, grads):
        terms = [
            jnp.dot(g, kt_ref[k], preferred_element_type=jnp.float32)
            for g, (k, _, _) in zip(grads, ids)
        ]
        for (_, _, b), term in zip(ids, terms):
            acc_in[b] += term

    return update


def weight_kernel(inner_ref, inner_live_ref, outer_ref, outer_live_ref, local_ref, received_ref, ft_ref, acc_w):
    acc_w[...] = jnp.zeros_like(acc_w)
    update = weight_updater(ft_ref, acc_w)
    pair_loop(inner_ref, inner_live_ref, local_ref, 0, update)
    pair_loop(outer_ref, outer_live_ref, received_ref, NB, update)


def input_kernel(inner_ref, inner_live_ref, outer_ref, outer_live_ref, local_ref, received_ref, kt_ref, after_ref, grad_out, acc_in):
    acc_in[...] = jnp.zeros_like(acc_in)
    update = input_updater(kt_ref, acc_in)
    pair_loop(inner_ref, inner_live_ref, local_ref, 0, update)
    pair_loop(outer_ref, outer_live_ref, received_ref, NB, update)
    grad_out[...] = acc_in[...].astype(grad_out.dtype)


def vmem():
    return pl.BlockSpec(memory_space=pltpu.MemorySpace.VMEM)


def smem():
    return pl.BlockSpec(memory_space=pltpu.MemorySpace.SMEM)


def cost(pairs):
    return pl.CostEstimate(
        flops=2 * pairs * BLOCK * C * C, transcendentals=0, bytes_accessed=6 * 1024 * 1024
    )


def run_weights(inner_pairs, inner_n, outer_pairs, outer_n, local, received, ft):
    return pl.pallas_call(
        weight_kernel,
        out_shape=jax.ShapeDtypeStruct((27, C, C), jnp.float32),
        in_specs=[smem(), smem(), smem(), smem(), vmem(), vmem(), vmem()],
        out_specs=vmem(),
        cost_estimate=cost(PI + PB),
        name="weight_pairs",
    )(inner_pairs, inner_n, outer_pairs, outer_n, local, received, ft)


def run_inputs(inner_pairs, inner_n, outer_pairs, outer_n, local, received, kt, after):
    return pl.pallas_call(
        input_kernel,
        out_shape=jax.ShapeDtypeStruct((NB, BLOCK, C), jnp.bfloat16),
        in_specs=[smem(), smem(), smem(), smem(), vmem(), vmem(), vmem(), vmem()],
        out_specs=vmem(),
        scratch_shapes=[pltpu.VMEM((NB, BLOCK, C), jnp.float32)],
        cost_estimate=cost(PI + PB),
        name="input_pairs",
    )(inner_pairs, inner_n, outer_pairs, outer_n, local, received, kt, after)


def reduce_weights(weight_acc, grad_scale):
    flat = weight_acc.reshape(-1)
    for axis in (GY, "x", ZZ):
        n = lax.axis_size(axis)
        parts = lax.all_to_all(flat.reshape(n, -1), axis, 0, 0, tiled=True)
        flat = parts.reshape(n, -1).sum(axis=0)
    after = flat
    piece = (flat * grad_scale).astype(jnp.bfloat16)
    n = lax.axis_size(ZZ)
    copies = jnp.broadcast_to(piece[None], (n,) + piece.shape)
    piece = lax.all_to_all(copies, ZZ, 0, 0, tiled=True).reshape(-1)
    piece = lax.all_gather(piece, "x", tiled=True)
    piece = lax.all_gather(piece, GY, tiled=True)
    return piece.reshape(weight_acc.shape), after


def body(features, output_grad, kernel, inner_map, outer_map, face_blocks, inner_live, outer_live):
    local_grads = output_grad[0, 0, 0].reshape(NB, BLOCK, C)
    feats_t = jnp.swapaxes(features[0, 0, 0].reshape(NB, BLOCK, C), 1, 2)
    kernel_t = jnp.swapaxes(kernel, 1, 2)
    inner_pairs = inner_map[0, 0, 0]
    outer_pairs = outer_map[0, 0, 0]
    inner_n = inner_live[0, 0]
    outer_n = outer_live[0, 0]
    received = received_blocks(local_grads, face_blocks[0, 0, 0])
    acc_w = run_weights(inner_pairs, inner_n, outer_pairs, outer_n, local_grads, received, feats_t)
    bricks_all = lax.axis_size(GX) * lax.axis_size(GY) * lax.axis_size("gz")
    grad_scale = math.sqrt(27.0 / (bricks_all * PI * BLOCK))
    weight_grad, after = reduce_weights(acc_w, grad_scale)
    input_grad = run_inputs(
        inner_pairs, inner_n, outer_pairs, outer_n, local_grads, received, kernel_t, after
    )
    return (input_grad.reshape(1, 1, 1, NB * BLOCK, C), weight_grad)


def solution(mesh):
    gx, gy, gz = (mesh.shape[name] for name in ("gx", "gy", "gz"))
    along_x = len({device.coords[0] for device in mesh.devices.flat})
    cores = gy // len({device.coords[1] for device in mesh.devices.flat})
    fine = Mesh(
        mesh.devices.reshape(gx // along_x, along_x, gy // cores, cores, gz),
        ("zh", "x", "y", "c", "gz"),
    )
    brick = P(GX, GY, "gz", None, None)
    in_specs = (
        brick,
        brick,
        P(),
        brick,
        brick,
        P(GX, GY, "gz", None, None, None),
        P(GX, GY, "gz"),
        P(GX, GY, "gz"),
    )
    out_specs = (brick, P())
    return jax.shard_map(body, mesh=fine, in_specs=in_specs, out_specs=out_specs, check_vma=False)
```

```python
import math

import jax
import jax.numpy as jnp
from jax import lax
from jax.experimental import pallas as pl
from jax.experimental.pallas import tpu as pltpu
from jax.sharding import Mesh
from jax.sharding import PartitionSpec as P

C = 128
BLOCK = 128
NB = 32
PI = 288
PB = 32
UNROLL = 16
GX = ("zh", "x")
GY = ("y", "c")
ZZ = ("zh", "gz")


def extended(shard, sides, width):
    for axis, dim in sides:
        count, length = (lax.axis_size(axis), shard.shape[dim])
        up = [(i, (i + 1) % count) for i in range(count - 1)]
        down = [(j, i) for i, j in up]
        last = lax.slice_in_dim(shard, length - width, length, axis=dim)
        initial = lax.slice_in_dim(shard, 0, width, axis=dim)
        before = lax.ppermute(last, axis, up)
        after = lax.ppermute(initial, axis, down)
        shard = jnp.concatenate([before, shard, after], axis=dim)
    return shard


def received_blocks(local_grads, face_lists):
    faces = local_grads[face_lists.reshape(-1)].reshape(3, 2, 4, BLOCK, C)
    got_x = extended(faces[0], ((GX, 0),), 1)
    got_y = extended(faces[1], ((GY, 0),), 1)
    got_z = extended(faces[2], (("gz", 0),), 1)
    return jnp.concatenate(
        [got_x[0], got_x[3], got_y[0], got_y[3], got_z[0], got_z[3]], axis=0
    )


def pair_loop(pairs_ref, live_ref, table_ref, table_base, update):
    def pair_ids(i):
        return (pairs_ref[i, 0], pairs_ref[i, 1] - table_base, pairs_ref[i, 2])

    live = jnp.clip(live_ref[0], 0, pairs_ref.shape[0])

    def group_at(group, masked):
        rows = [group * UNROLL + j for j in range(UNROLL)]
        ids = [pair_ids(row) for row in rows]
        grads = [table_ref[a] for _, a, _ in ids]
        update(ids, grads, [row < live for row in rows] if masked else None)

    def one_group(group, carry):
        group_at(group, False)
        return carry

    def last_group(group, carry):
        group_at(group, True)
        return carry

    groups = live // UNROLL
    lax.fori_loop(0, groups, one_group, 0)
    lax.fori_loop(groups, (live + UNROLL - 1) // UNROLL, last_group, 0)


def keep(term, valid):
    return term if valid is None else jnp.where(valid, term, jnp.zeros_like(term))


def weight_updater(ft_ref, acc_w):
    def update(ids, grads, valid):
        terms = [
            jnp.dot(ft_ref[b], g, preferred_element_type=jnp.float32)
            for g, (_, _, b) in zip(grads, ids)
        ]
        for j, ((k, _, _), term) in enumerate(zip(ids, terms)):
            acc_w[k] += keep(term, None if valid is None else valid[j])

    return update


def input_updater(kt_ref, acc_in):
    def update(ids, grads, valid):
        terms = [
            jnp.dot(g, kt_ref[k], preferred_element_type=jnp.float32)
            for g, (k, _, _) in zip(grads, ids)
        ]
        for j, ((_, _, b), term) in enumerate(zip(ids, terms)):
            acc_in[b] += keep(term, None if valid is None else valid[j])

    return update


def weight_kernel(inner_ref, inner_live_ref, outer_ref, outer_live_ref, local_ref, received_ref, ft_ref, acc_w):
    acc_w[...] = jnp.zeros_like(acc_w)
    update = weight_updater(ft_ref, acc_w)
    pair_loop(inner_ref, inner_live_ref, local_ref, 0, update)
    pair_loop(outer_ref, outer_live_ref, received_ref, NB, update)


def input_kernel(inner_ref, inner_live_ref, outer_ref, outer_live_ref, local_ref, received_ref, kt_ref, after_ref, grad_out, acc_in):
    acc_in[...] = jnp.zeros_like(acc_in)
    update = input_updater(kt_ref, acc_in)
    pair_loop(inner_ref, inner_live_ref, local_ref, 0, update)
    pair_loop(outer_ref, outer_live_ref, received_ref, NB, update)
    grad_out[...] = acc_in[...].astype(grad_out.dtype)


def vmem():
    return pl.BlockSpec(memory_space=pltpu.MemorySpace.VMEM)


def smem():
    return pl.BlockSpec(memory_space=pltpu.MemorySpace.SMEM)


def cost(pairs):
    return pl.CostEstimate(
        flops=2 * pairs * BLOCK * C * C, transcendentals=0, bytes_accessed=6 * 1024 * 1024
    )


def run_weights(inner_pairs, inner_n, outer_pairs, outer_n, local, received, ft):
    return pl.pallas_call(
        weight_kernel,
        out_shape=jax.ShapeDtypeStruct((27, C, C), jnp.float32),
        in_specs=[smem(), smem(), smem(), smem(), vmem(), vmem(), vmem()],
        out_specs=vmem(),
        cost_estimate=cost(PI + PB),
        name="weight_pairs",
    )(inner_pairs, inner_n, outer_pairs, outer_n, local, received, ft)


def run_inputs(inner_pairs, inner_n, outer_pairs, outer_n, local, received, kt, after):
    return pl.pallas_call(
        input_kernel,
        out_shape=jax.ShapeDtypeStruct((NB, BLOCK, C), jnp.bfloat16),
        in_specs=[smem(), smem(), smem(), smem(), vmem(), vmem(), vmem(), vmem()],
        out_specs=vmem(),
        scratch_shapes=[pltpu.VMEM((NB, BLOCK, C), jnp.float32)],
        cost_estimate=cost(PI + PB),
        name="input_pairs",
    )(inner_pairs, inner_n, outer_pairs, outer_n, local, received, kt, after)


def reduce_weights(weight_acc, grad_scale):
    flat = weight_acc.reshape(-1)
    for axis in (GY, "x", ZZ):
        n = lax.axis_size(axis)
        parts = lax.all_to_all(flat.reshape(n, -1), axis, 0, 0, tiled=True)
        flat = parts.reshape(n, -1).sum(axis=0)
    after = flat
    piece = (flat * grad_scale).astype(jnp.bfloat16)
    n = lax.axis_size(ZZ)
    copies = jnp.broadcast_to(piece[None], (n,) + piece.shape)
    piece = lax.all_to_all(copies, ZZ, 0, 0, tiled=True).reshape(-1)
    piece = lax.all_gather(piece, "x", tiled=True)
    piece = lax.all_gather(piece, GY, tiled=True)
    return piece.reshape(weight_acc.shape), after


def body(features, output_grad, kernel, inner_map, outer_map, face_blocks, inner_live, outer_live):
    local_grads = output_grad[0, 0, 0].reshape(NB, BLOCK, C)
    feats_t = jnp.swapaxes(features[0, 0, 0].reshape(NB, BLOCK, C), 1, 2)
    kernel_t = jnp.swapaxes(kernel, 1, 2)
    inner_pairs = inner_map[0, 0, 0]
    outer_pairs = outer_map[0, 0, 0]
    inner_n = inner_live[0, 0]
    outer_n = outer_live[0, 0]
    received = received_blocks(local_grads, face_blocks[0, 0, 0])
    acc_w = run_weights(inner_pairs, inner_n, outer_pairs, outer_n, local_grads, received, feats_t)
    bricks_all = lax.axis_size(GX) * lax.axis_size(GY) * lax.axis_size("gz")
    grad_scale = math.sqrt(27.0 / (bricks_all * PI * BLOCK))
    weight_grad, after = reduce_weights(acc_w, grad_scale)
    input_grad = run_inputs(
        inner_pairs, inner_n, outer_pairs, outer_n, local_grads, received, kernel_t, after
    )
    return (input_grad.reshape(1, 1, 1, NB * BLOCK, C), weight_grad)


def solution(mesh):
    gx, gy, gz = (mesh.shape[name] for name in ("gx", "gy", "gz"))
    along_x = len({device.coords[0] for device in mesh.devices.flat})
    cores = gy // len({device.coords[1] for device in mesh.devices.flat})
    fine = Mesh(
        mesh.devices.reshape(gx // along_x, along_x, gy // cores, cores, gz),
        ("zh", "x", "y", "c", "gz"),
    )
    brick = P(GX, GY, "gz", None, None)
    in_specs = (
        brick,
        brick,
        P(),
        brick,
        brick,
        P(GX, GY, "gz", None, None, None),
        P(GX, GY, "gz"),
        P(GX, GY, "gz"),
    )
    out_specs = (brick, P())
    return jax.shard_map(body, mesh=fine, in_specs=in_specs, out_specs=out_specs, check_vma=False)
```

```python
import math

import jax
import jax.numpy as jnp
from jax import lax
from jax.experimental import pallas as pl
from jax.experimental.pallas import tpu as pltpu
from jax.sharding import Mesh
from jax.sharding import PartitionSpec as P

C = 128
BLOCK = 128
NB = 32
PI = 288
PB = 32
UNROLL = 16
GX = ("zh", "x")
GY = ("y", "c")
ZZ = ("zh", "gz")


def extended(shard, sides, width):
    for axis, dim in sides:
        count, length = (lax.axis_size(axis), shard.shape[dim])
        up = [(i, (i + 1) % count) for i in range(count - 1)]
        down = [(j, i) for i, j in up]
        last = lax.slice_in_dim(shard, length - width, length, axis=dim)
        initial = lax.slice_in_dim(shard, 0, width, axis=dim)
        before = lax.ppermute(last, axis, up)
        after = lax.ppermute(initial, axis, down)
        shard = jnp.concatenate([before, shard, after], axis=dim)
    return shard


def received_blocks(local_grads, face_lists):
    faces = local_grads[face_lists.reshape(-1)].reshape(3, 2, 4, BLOCK, C)
    got_x = extended(faces[0], ((GX, 0),), 1)
    got_y = extended(faces[1], ((GY, 0),), 1)
    got_z = extended(faces[2], (("gz", 0),), 1)
    return jnp.concatenate(
        [got_x[0], got_x[3], got_y[0], got_y[3], got_z[0], got_z[3]], axis=0
    )


def pair_loop(pairs_ref, live_ref, table_ref, table_base, update):
    def pair_ids(i):
        return (pairs_ref[i, 0], pairs_ref[i, 1] - table_base, pairs_ref[i, 2])

    live = jnp.clip(live_ref[0], 0, pairs_ref.shape[0])

    def group_at(group, masked):
        rows = [group * UNROLL + j for j in range(UNROLL)]
        ids = [pair_ids(row) for row in rows]
        grads = [table_ref[a] for _, a, _ in ids]
        update(ids, grads, [row < live for row in rows] if masked else None)

    def one_group(group, carry):
        group_at(group, False)
        return carry

    def last_group(group, carry):
        group_at(group, True)
        return carry

    groups = live // UNROLL
    lax.fori_loop(0, groups, one_group, 0)
    lax.fori_loop(groups, (live + UNROLL - 1) // UNROLL, last_group, 0)


def keep(term, valid):
    return term if valid is None else jnp.where(valid, term, jnp.zeros_like(term))


def weight_updater(ft_ref, acc_w):
    def update(ids, grads, valid):
        terms = [
            jnp.dot(ft_ref[b], g, preferred_element_type=jnp.float32)
            for g, (_, _, b) in zip(grads, ids)
        ]
        for j, ((k, _, _), term) in enumerate(zip(ids, terms)):
            acc_w[k] += keep(term, None if valid is None else valid[j])

    return update


def input_updater(kt_ref, acc_in):
    def update(ids, grads, valid):
        terms = [
            jnp.dot(g, kt_ref[k], preferred_element_type=jnp.float32)
            for g, (k, _, _) in zip(grads, ids)
        ]
        for j, ((_, _, b), term) in enumerate(zip(ids, terms)):
            acc_in[b] += keep(term, None if valid is None else valid[j])

    return update


def weight_kernel(inner_ref, inner_live_ref, outer_ref, outer_live_ref, local_ref, received_ref, f_ref, acc_w, ft_ref):
    def transpose_block(b, carry):
        ft_ref[b] = f_ref[b].T
        return carry

    lax.fori_loop(0, NB, transpose_block, 0)
    acc_w[...] = jnp.zeros_like(acc_w)
    update = weight_updater(ft_ref, acc_w)
    pair_loop(inner_ref, inner_live_ref, local_ref, 0, update)
    pair_loop(outer_ref, outer_live_ref, received_ref, NB, update)


def input_kernel(inner_ref, inner_live_ref, outer_ref, outer_live_ref, local_ref, received_ref, kt_ref, after_ref, grad_out, acc_in):
    acc_in[...] = jnp.zeros_like(acc_in)
    update = input_updater(kt_ref, acc_in)
    pair_loop(inner_ref, inner_live_ref, local_ref, 0, update)
    pair_loop(outer_ref, outer_live_ref, received_ref, NB, update)
    grad_out[...] = acc_in[...].astype(grad_out.dtype)


def vmem():
    return pl.BlockSpec(memory_space=pltpu.MemorySpace.VMEM)


def smem():
    return pl.BlockSpec(memory_space=pltpu.MemorySpace.SMEM)


def cost(pairs):
    return pl.CostEstimate(
        flops=2 * pairs * BLOCK * C * C, transcendentals=0, bytes_accessed=6 * 1024 * 1024
    )


def run_weights(inner_pairs, inner_n, outer_pairs, outer_n, local, received, ft):
    return pl.pallas_call(
        weight_kernel,
        out_shape=jax.ShapeDtypeStruct((27, C, C), jnp.float32),
        in_specs=[smem(), smem(), smem(), smem(), vmem(), vmem(), vmem()],
        out_specs=vmem(),
        scratch_shapes=[pltpu.VMEM((NB, C, BLOCK), jnp.bfloat16)],
        cost_estimate=cost(PI + PB),
        name="weight_pairs",
    )(inner_pairs, inner_n, outer_pairs, outer_n, local, received, ft)


def run_inputs(inner_pairs, inner_n, outer_pairs, outer_n, local, received, kt, after):
    return pl.pallas_call(
        input_kernel,
        out_shape=jax.ShapeDtypeStruct((NB, BLOCK, C), jnp.bfloat16),
        in_specs=[smem(), smem(), smem(), smem(), vmem(), vmem(), vmem(), vmem()],
        out_specs=vmem(),
        scratch_shapes=[pltpu.VMEM((NB, BLOCK, C), jnp.float32)],
        cost_estimate=cost(PI + PB),
        name="input_pairs",
    )(inner_pairs, inner_n, outer_pairs, outer_n, local, received, kt, after)


def reduce_weights(weight_acc, grad_scale):
    flat = weight_acc.reshape(-1)
    for axis in (GY, "x", ZZ):
        n = lax.axis_size(axis)
        parts = lax.all_to_all(flat.reshape(n, -1), axis, 0, 0, tiled=True)
        flat = parts.reshape(n, -1).sum(axis=0)
    after = flat
    piece = (flat * grad_scale).astype(jnp.bfloat16)
    n = lax.axis_size(ZZ)
    copies = jnp.broadcast_to(piece[None], (n,) + piece.shape)
    piece = lax.all_to_all(copies, ZZ, 0, 0, tiled=True).reshape(-1)
    piece = lax.all_gather(piece, "x", tiled=True)
    piece = lax.all_gather(piece, GY, tiled=True)
    return piece.reshape(weight_acc.shape), after


def body(features, output_grad, kernel, inner_map, outer_map, face_blocks, inner_live, outer_live):
    local_grads = output_grad[0, 0, 0].reshape(NB, BLOCK, C)
    feats = features[0, 0, 0].reshape(NB, BLOCK, C)
    kernel_t = jnp.swapaxes(kernel, 1, 2)
    inner_pairs = inner_map[0, 0, 0]
    outer_pairs = outer_map[0, 0, 0]
    inner_n = inner_live[0, 0]
    outer_n = outer_live[0, 0]
    received = received_blocks(local_grads, face_blocks[0, 0, 0])
    acc_w = run_weights(inner_pairs, inner_n, outer_pairs, outer_n, local_grads, received, feats)
    bricks_all = lax.axis_size(GX) * lax.axis_size(GY) * lax.axis_size("gz")
    grad_scale = math.sqrt(27.0 / (bricks_all * PI * BLOCK))
    weight_grad, after = reduce_weights(acc_w, grad_scale)
    input_grad = run_inputs(
        inner_pairs, inner_n, outer_pairs, outer_n, local_grads, received, kernel_t, after
    )
    return (input_grad.reshape(1, 1, 1, NB * BLOCK, C), weight_grad)


def solution(mesh):
    gx, gy, gz = (mesh.shape[name] for name in ("gx", "gy", "gz"))
    along_x = len({device.coords[0] for device in mesh.devices.flat})
    cores = gy // len({device.coords[1] for device in mesh.devices.flat})
    fine = Mesh(
        mesh.devices.reshape(gx // along_x, along_x, gy // cores, cores, gz),
        ("zh", "x", "y", "c", "gz"),
    )
    brick = P(GX, GY, "gz", None, None)
    in_specs = (
        brick,
        brick,
        P(),
        brick,
        brick,
        P(GX, GY, "gz", None, None, None),
        P(GX, GY, "gz"),
        P(GX, GY, "gz"),
    )
    out_specs = (brick, P())
    return jax.shard_map(body, mesh=fine, in_specs=in_specs, out_specs=out_specs, check_vma=False)
```
